768 devices in a mesh: rows: 384 (over x, z, y_lo, core), rep: 2 (over y_hi).
Axes of the slice: x: 4, y: 8 (y_hi: 2, y_lo: 4; y = y_hi * 4 + y_lo), z: 12, core: 2. Of those that a mesh axis runs over, the one named last changes fastest.
Arguments:
- features: bfloat16 [294912, 256], P('rows'), may hold values from -6 to 6
- tiles: bfloat16 [2304, 12, 128, 128], P('rows', 'rep'), may hold values from -0.21875 to 0.21875
- columns: int32 [2304, 12], P('rows', 'rep'), may hold values from 0 to 2303, as said below
- live: int32 [2304, 2], P('rows', 'rep'), may hold values from 1 to 6, as said below
- weight: bfloat16 [256, 256], replicated, may hold values from -0.375 to 0.375
- bias: float32 [256], replicated, may hold values from -3 to 3
- cotangent: bfloat16 [294912, 256], P('rows'), may hold values from -6 to 6
Outputs:
- activations: bfloat16 [294912, 256], P('rows')
- feature_grad: bfloat16 [294912, 256], P('rows')
- weight_grad: float32 [256, 256], replicated
- bias_grad: float32 [256], replicated
The draws below stay inside these ranges and needn't reach their ends.
Inputs may be any that keep to these rules, and one draw needn't show every extreme that they name: `columns`: the 12 slots of row block g name, in some order, each of the blocks s to s + 2 * 6 - 1 once, where s = g - 6 clipped to 0 .. 2292. `live`: 1 to 6 live slots in each half of a row block's slots; some row block in every draw has all 6 live in its first half.
All inputs are finite; a program needn't handle non-finite values.
Results may differ from the reference program's by a relative error of at most 0.0061.
Values may be sent and summed in bfloat16 or wider, within the bound.
No kernel may reach another device: no remote copies, remote signals or barrier semaphores. Data moves between devices by JAX's collectives and lax.ppermute only.
A program may use at most 32 MiB of HBM per device.

```python
import math
import jax
import jax.numpy as jnp
from jax import lax

F = 256
TILE = 128
NB = 6
SLOTS = 6
NBLOCKS = 2304
NODES = 294912
N_ROWS = 384


def draw_columns(key, part):
    block_ids = jnp.arange(NBLOCKS, dtype=jnp.int32)
    window_start = jnp.clip(block_ids - NB, 0, NBLOCKS - 2 * NB)
    row_keys = jax.random.split(key, NBLOCKS)
    orders = jax.vmap(lambda one_key: jax.random.permutation(one_key, 2 * NB))(row_keys)
    return (window_start[:, None] + orders.astype(jnp.int32)).astype(jnp.int32)


def draw_live(key, part):
    counts = jax.random.randint(key, (NBLOCKS, 2), 1, SLOTS + 1, dtype=jnp.int32)
    block_ids = jnp.arange(NBLOCKS, dtype=jnp.int32)
    first_half = jnp.where(block_ids % 4 == 0, SLOTS, counts[:, 0])
    return counts.at[:, 0].set(first_half).astype(jnp.int32)


def block_levels(stream_key, shape, cuts, smallest, high):
    loudness, own = 1.0, jax.random.fold_in(stream_key, 6)
    for position, shards_of in cuts:
        draws = jnp.exp(jax.random.uniform(jax.random.fold_in(own, position), (shards_of,), jnp.float32, smallest / len(cuts), high / len(cuts)))
        loudness = loudness * jnp.repeat(draws, shape[position] // shards_of).reshape([-1 if axis == position else 1 for axis in range(len(shape))])
    return loudness


def bell_draw(stream_key, extent, scale, most, pieces=(), kind=jnp.bfloat16):
    array = jax.random.normal(stream_key, extent, jnp.float32) * scale
    if len(pieces) > 0:
        array = block_levels(stream_key, extent, pieces, -0.22, 0.18) * array
    return jnp.clip(array, min=-most, max=most).astype(kind)


def setup_inputs(seed: int = 0) -> dict:
    arg_keys = jax.random.split(jax.random.key(seed), 8)
    features = bell_draw(arg_keys[0], (NODES, F), 1.0, 6.0, ((0, 384),))
    tiles = bell_draw(arg_keys[1], (NBLOCKS, 2 * SLOTS, TILE, TILE), (TILE * SLOTS) ** -0.5, 0.21875, ((0, 384), (1, 2)))
    columns = draw_columns(jax.random.fold_in(arg_keys[7], 71), 0)
    live = draw_live(jax.random.fold_in(arg_keys[7], 71), 0)
    weight = bell_draw(arg_keys[4], (F, F), F ** -0.5, 0.375)
    bias = bell_draw(arg_keys[5], (F,), 0.5, 3.0, (), jnp.float32)
    cotangent = bell_draw(arg_keys[6], (NODES, F), 1.0, 6.0, ((0, 384),))
    return dict(features=features, tiles=tiles, columns=columns, live=live, weight=weight, bias=bias, cotangent=cotangent)


def reference(features, tiles, columns, live, weight, bias, cotangent):
    node_count = features.shape[0]
    block_count = columns.shape[0]
    tile_size = tiles.shape[2]
    slot_total = columns.shape[1]
    slot_ids = jnp.arange(slot_total, dtype=jnp.int32)
    half_index = slot_ids // SLOTS
    within = slot_ids % SLOTS
    live_mask = within[None, :] < live[:, half_index]
    feat_blocks = features.reshape(block_count, tile_size, F)

    def aggregate_group(group):
        start = (group * NB).astype(jnp.int32)
        tile_part = lax.dynamic_slice_in_dim(tiles, start, NB, 0)
        col_part = lax.dynamic_slice_in_dim(columns, start, NB, 0)
        mask_part = lax.dynamic_slice_in_dim(live_mask, start, NB, 0)
        gathered = feat_blocks[col_part] * mask_part[:, :, None, None].astype(jnp.bfloat16)
        return jnp.einsum('bkij,bkjf->bif', tile_part.astype(jnp.float32), gathered.astype(jnp.float32))
    aggregate = lax.map(aggregate_group, jnp.arange(N_ROWS, dtype=jnp.int32))
    aggregate = aggregate.reshape(node_count, F).astype(jnp.bfloat16)
    pre_act = jnp.dot(aggregate, weight, preferred_element_type=jnp.float32) + bias
    activations = jax.nn.silu(pre_act).astype(jnp.bfloat16)
    sigmoid_pre = jax.nn.sigmoid(pre_act)
    pre_grad = (cotangent.astype(jnp.float32) * sigmoid_pre * (1.0 + pre_act * (1.0 - sigmoid_pre))).astype(jnp.bfloat16)
    agg_grad = jnp.dot(pre_grad, weight.T, preferred_element_type=jnp.float32).astype(jnp.bfloat16)
    grad_blocks = agg_grad.reshape(block_count, tile_size, F)

    def spread_group(buffer, group):
        start = (group * NB).astype(jnp.int32)
        tile_part = lax.dynamic_slice_in_dim(tiles, start, NB, 0)
        col_part = lax.dynamic_slice_in_dim(columns, start, NB, 0)
        mask_part = lax.dynamic_slice_in_dim(live_mask, start, NB, 0)
        grad_part = lax.dynamic_slice_in_dim(grad_blocks, start, NB, 0)
        contrib = jnp.einsum('bkij,bif->bkjf', tile_part.astype(jnp.float32), grad_part.astype(jnp.float32))
        contrib = contrib * mask_part[:, :, None, None].astype(jnp.float32)
        buffer = buffer.at[col_part.reshape(-1)].add(contrib.reshape(-1, tile_size, F))
        return (buffer, None)
    buffer = jnp.zeros((block_count, tile_size, F), jnp.float32)
    buffer, unused = lax.scan(spread_group, buffer, jnp.arange(N_ROWS, dtype=jnp.int32))
    feature_grad = buffer.reshape(node_count, F).astype(jnp.bfloat16)
    scale = 1.0 / math.sqrt(node_count)
    weight_grad = jnp.dot(aggregate.T, pre_grad, preferred_element_type=jnp.float32) * scale
    bias_grad = lax.optimization_barrier(jnp.sum(pre_grad.astype(jnp.float32), axis=0)) * scale
    return (activations, feature_grad, weight_grad, bias_grad)
```

```python
import math

import jax
import jax.numpy as jnp
from jax import lax
from jax.sharding import PartitionSpec as P


def extended(block, sides, width):
    for axis, dim in sides:
        count = lax.axis_size(axis)
        forward = [(i, i + 1) for i in range(count - 1)]
        backward = [(target, source) for source, target in forward]
        low = lax.ppermute(
            lax.slice_in_dim(block, block.shape[dim] - width, None, axis=dim), axis, forward
        )
        high = lax.ppermute(lax.slice_in_dim(block, 0, width, axis=dim), axis, backward)
        block = jnp.concatenate([low, block, high], axis=dim)
    return block


def from_behind(x, axis, by):
    count = lax.axis_size(axis)
    pairs = [(i, i + by) for i in range(count) if 0 <= i + by < count]
    return lax.ppermute(x, axis, pairs)


ROW_AXES = {384: ((96, 4), (8, 12), (2, 4), (1, 2))}


def moved(x, axis, count, stride, size, target):
    pairs = []
    for index in range(count):
        coord = (index // stride) % size
        pairs.append((index, index + (target(coord) - coord) * stride))
    return lax.ppermute(x, axis, pairs)


def swapped_sum(x, axis, count, stride, size, bit):
    return x + moved(x, axis, count, stride, size, lambda c: c ^ bit)


def three_way_sum(x, axis, count, stride, size):
    third = size // 3
    ahead = moved(x, axis, count, stride, size, lambda c: (c + third) % size)
    behind = moved(x, axis, count, stride, size, lambda c: (c - third) % size)
    group = (lax.axis_index(axis) // stride) % size // third
    first = jnp.where(group == 0, x, jnp.where(group == 1, ahead, behind))
    second = jnp.where(group == 0, behind, jnp.where(group == 1, x, ahead))
    third_part = jnp.where(group == 0, ahead, jnp.where(group == 1, behind, x))
    return (first + second) + third_part


def global_sum(x):
    count = lax.axis_size("rows")
    if count not in ROW_AXES or lax.axis_size("rep") != 2:
        return lax.psum(x, ("rows", "rep"))
    (x_stride, x_size), (z_stride, z_size), (y_stride, y_size), (c_stride, c_size) = ROW_AXES[count]
    x = swapped_sum(x, "rows", count, c_stride, c_size, 1)
    x = swapped_sum(x, "rows", count, y_stride, y_size, 1)
    x = swapped_sum(x, "rows", count, y_stride, y_size, 2)
    x = x + lax.ppermute(x, "rep", [(0, 1), (1, 0)])
    x = swapped_sum(x, "rows", count, x_stride, x_size, 1)
    x = swapped_sum(x, "rows", count, x_stride, x_size, 2)
    x = swapped_sum(x, "rows", count, z_stride, z_size, 1)
    x = swapped_sum(x, "rows", count, z_stride, z_size, 2)
    return three_way_sum(x, "rows", count, z_stride, z_size)


def partner_sum(x):
    return x + lax.ppermute(x, "rep", [(0, 1), (1, 0)])


def dense_part(aggregated, grad_input, weight, bias):
    pre_act = jnp.dot(aggregated, weight, preferred_element_type=jnp.float32) + bias
    outputs = jax.nn.silu(pre_act).astype(jnp.bfloat16)
    sigmoid_pre = jax.nn.sigmoid(pre_act)
    pre_grad = (
        grad_input.astype(jnp.float32) * sigmoid_pre * (1.0 + pre_act * (1.0 - sigmoid_pre))
    ).astype(jnp.bfloat16)
    agg_grad = jnp.dot(pre_grad, weight.T, preferred_element_type=jnp.float32).astype(jnp.bfloat16)
    return (outputs, pre_grad, agg_grad)


def local(features, tiles, columns, live, weight, bias, cotangent):
    num_blocks = tiles.shape[0]
    slot_count = tiles.shape[1]
    tile_size = tiles.shape[2]
    feat_width = features.shape[1]
    rows_here = num_blocks * tile_size
    half_rows = rows_here // 2
    row_index = lax.axis_index("rows")
    partner = lax.axis_index("rep")
    node_count = rows_here * lax.axis_size("rows")
    padded = extended(features, (("rows", 0),), rows_here)
    padded_blocks = padded.reshape(3 * num_blocks, tile_size, feat_width)
    local_cols = columns - (row_index - 1) * num_blocks
    live_mask = jnp.arange(slot_count, dtype=jnp.int32)[None, :] < live
    targets = jnp.arange(3 * num_blocks, dtype=jnp.int32)
    selector = (local_cols[:, :, None] == targets[None, None, :]) & live_mask[:, :, None]
    selector = selector.astype(jnp.bfloat16)
    band_tiles = jnp.einsum(
        "bks,bkij->bsij", selector, tiles, preferred_element_type=jnp.float32
    ).astype(jnp.bfloat16)
    partial_sum = jnp.einsum(
        "bsij,sjf->bif", band_tiles, padded_blocks, preferred_element_type=jnp.float32
    )
    partial_sum = partial_sum.reshape(rows_here, feat_width)
    aggregate = partner_sum(partial_sum).astype(jnp.bfloat16)
    activations, pre_grad, agg_grad = dense_part(aggregate, cotangent, weight, bias)
    agg_half = lax.dynamic_slice_in_dim(aggregate, partner * half_rows, half_rows, 0)
    grad_half = lax.dynamic_slice_in_dim(pre_grad, partner * half_rows, half_rows, 0)
    weight_part = lax.dot_general(
        agg_half, grad_half, (((0,), (0,)), ((), ())), preferred_element_type=jnp.float32
    )
    bias_part = jnp.sum(grad_half.astype(jnp.float32), axis=0)
    grad_terms = global_sum(jnp.concatenate([weight_part, bias_part[None, :]], axis=0))
    weight_total = grad_terms[:feat_width]
    bias_total = grad_terms[feat_width]
    scale = 1.0 / math.sqrt(node_count)
    weight_grad = weight_total * scale
    bias_grad = bias_total * scale
    grad_blocks = agg_grad.reshape(num_blocks, tile_size, feat_width)
    spread = jnp.einsum(
        "bsij,bif->sjf", band_tiles, grad_blocks, preferred_element_type=jnp.float32
    )
    from_above = from_behind(spread[:num_blocks], "rows", -1)
    from_below = from_behind(spread[2 * num_blocks :].astype(jnp.bfloat16), "rows", 1).astype(
        jnp.float32
    )
    own_terms = spread[num_blocks : 2 * num_blocks] + from_above + from_below
    own_total = partner_sum(own_terms)
    feature_grad = own_total.reshape(rows_here, feat_width).astype(jnp.bfloat16)
    return (activations, feature_grad, weight_grad, bias_grad)


def solution(mesh):
    placed = (
        P("rows", None),
        P("rows", "rep", None, None),
        P("rows", "rep"),
        P("rows", "rep"),
        P(),
        P(),
        P("rows", None),
    )
    return jax.shard_map(
        local,
        mesh=mesh,
        in_specs=placed,
        out_specs=(P("rows", None), P("rows", None), P(), P()),
        check_vma=False,
    )
```

```python
import math

import jax
import jax.numpy as jnp
from jax import lax
from jax.sharding import PartitionSpec as P


def extended(block, sides, width):
    for axis, dim in sides:
        count = lax.axis_size(axis)
        forward = [(i, i + 1) for i in range(count - 1)]
        backward = [(target, source) for source, target in forward]
        low = lax.ppermute(
            lax.slice_in_dim(block, block.shape[dim] - width, None, axis=dim), axis, forward
        )
        high = lax.ppermute(lax.slice_in_dim(block, 0, width, axis=dim), axis, backward)
        block = jnp.concatenate([low, block, high], axis=dim)
    return block


def from_behind(x, axis, by):
    count = lax.axis_size(axis)
    pairs = [(i, i + by) for i in range(count) if 0 <= i + by < count]
    return lax.ppermute(x, axis, pairs)


ROW_AXES = {384: ((96, 4), (8, 12), (2, 4), (1, 2))}


def moved(x, axis, count, stride, size, target):
    pairs = []
    for index in range(count):
        coord = (index // stride) % size
        pairs.append((index, index + (target(coord) - coord) * stride))
    return lax.ppermute(x, axis, pairs)


def swapped_sum(x, axis, count, stride, size, bit):
    return x + moved(x, axis, count, stride, size, lambda c: c ^ bit)


def three_way_sum(x, axis, count, stride, size):
    third = size // 3
    ahead = moved(x, axis, count, stride, size, lambda c: (c + third) % size)
    behind = moved(x, axis, count, stride, size, lambda c: (c - third) % size)
    group = (lax.axis_index(axis) // stride) % size // third
    first = jnp.where(group == 0, x, jnp.where(group == 1, ahead, behind))
    second = jnp.where(group == 0, behind, jnp.where(group == 1, x, ahead))
    third_part = jnp.where(group == 0, ahead, jnp.where(group == 1, behind, x))
    return (first + second) + third_part


def global_sum(x):
    count = lax.axis_size("rows")
    if count not in ROW_AXES or lax.axis_size("rep") != 2:
        return lax.psum(x, ("rows", "rep"))
    (x_stride, x_size), (z_stride, z_size), (y_stride, y_size), (c_stride, c_size) = ROW_AXES[count]
    core = (lax.axis_index("rows") // c_stride) % c_size
    width = x.shape[1] // 2
    keep = lax.dynamic_slice_in_dim(x, core * width, width, 1)
    give = lax.dynamic_slice_in_dim(x, (1 - core) * width, width, 1)
    x = keep + moved(give, "rows", count, c_stride, c_size, lambda c: c ^ 1)
    x = swapped_sum(x, "rows", count, y_stride, y_size, 1)
    x = swapped_sum(x, "rows", count, y_stride, y_size, 2)
    x = x + lax.ppermute(x, "rep", [(0, 1), (1, 0)])
    x = swapped_sum(x, "rows", count, x_stride, x_size, 1)
    x = swapped_sum(x, "rows", count, x_stride, x_size, 2)
    x = swapped_sum(x, "rows", count, z_stride, z_size, 1)
    x = swapped_sum(x, "rows", count, z_stride, z_size, 2)
    x = three_way_sum(x, "rows", count, z_stride, z_size)
    other = moved(x, "rows", count, c_stride, c_size, lambda c: c ^ 1)
    return jnp.where(core == 0, jnp.concatenate([x, other], 1), jnp.concatenate([other, x], 1))


def partner_swap(x):
    return lax.ppermute(x, "rep", [(0, 1), (1, 0)])


def in_order(mine, theirs, partner):
    return jnp.where(
        partner == 0, jnp.concatenate([mine, theirs], 0), jnp.concatenate([theirs, mine], 0)
    )


def partner_sum(x):
    return x + lax.ppermute(x, "rep", [(0, 1), (1, 0)])


def dense_part(aggregated, grad_input, weight, bias):
    pre_act = jnp.dot(aggregated, weight, preferred_element_type=jnp.float32) + bias
    outputs = jax.nn.silu(pre_act).astype(jnp.bfloat16)
    sigmoid_pre = jax.nn.sigmoid(pre_act)
    pre_grad = (
        grad_input.astype(jnp.float32) * sigmoid_pre * (1.0 + pre_act * (1.0 - sigmoid_pre))
    ).astype(jnp.bfloat16)
    agg_grad = jnp.dot(pre_grad, weight.T, preferred_element_type=jnp.float32).astype(jnp.bfloat16)
    return (outputs, pre_grad, agg_grad)


def local(features, tiles, columns, live, weight, bias, cotangent):
    num_blocks = tiles.shape[0]
    slot_count = tiles.shape[1]
    tile_size = tiles.shape[2]
    feat_width = features.shape[1]
    rows_here = num_blocks * tile_size
    half_rows = rows_here // 2
    row_index = lax.axis_index("rows")
    partner = lax.axis_index("rep")
    node_count = rows_here * lax.axis_size("rows")
    padded = extended(features, (("rows", 0),), rows_here)
    padded_blocks = padded.reshape(3 * num_blocks, tile_size, feat_width)
    local_cols = columns - (row_index - 1) * num_blocks
    live_mask = jnp.arange(slot_count, dtype=jnp.int32)[None, :] < live
    targets = jnp.arange(3 * num_blocks, dtype=jnp.int32)
    selector = (local_cols[:, :, None] == targets[None, None, :]) & live_mask[:, :, None]
    selector = selector.astype(jnp.bfloat16)
    band_tiles = jnp.einsum(
        "bks,bkij->bsij", selector, tiles, preferred_element_type=jnp.float32
    ).astype(jnp.bfloat16)
    partial_sum = jnp.einsum(
        "bsij,sjf->bif", band_tiles, padded_blocks, preferred_element_type=jnp.float32
    )
    partial_sum = partial_sum.reshape(rows_here, feat_width)
    own_part = lax.dynamic_slice_in_dim(partial_sum, partner * half_rows, half_rows, 0)
    their_part = lax.dynamic_slice_in_dim(partial_sum, (1 - partner) * half_rows, half_rows, 0)
    agg_half = (own_part + partner_swap(their_part)).astype(jnp.bfloat16)
    grad_in = lax.dynamic_slice_in_dim(cotangent, partner * half_rows, half_rows, 0)
    act_half, grad_half, agg_grad_half = dense_part(agg_half, grad_in, weight, bias)
    sent = partner_swap(jnp.concatenate([act_half, agg_grad_half], 1))
    activations = in_order(act_half, sent[:, :feat_width], partner)
    agg_grad = in_order(agg_grad_half, sent[:, feat_width:], partner)
    weight_part = lax.dot_general(
        agg_half, grad_half, (((0,), (0,)), ((), ())), preferred_element_type=jnp.float32
    )
    bias_part = jnp.sum(grad_half.astype(jnp.float32), axis=0)
    grad_terms = global_sum(jnp.concatenate([weight_part, bias_part[None, :]], axis=0))
    weight_total = grad_terms[:feat_width]
    bias_total = grad_terms[feat_width]
    scale = 1.0 / math.sqrt(node_count)
    weight_grad = weight_total * scale
    bias_grad = bias_total * scale
    grad_blocks = agg_grad.reshape(num_blocks, tile_size, feat_width)
    spread = jnp.einsum(
        "bsij,bif->sjf", band_tiles, grad_blocks, preferred_element_type=jnp.float32
    )
    from_above = from_behind(spread[:num_blocks], "rows", -1)
    from_below = from_behind(spread[2 * num_blocks :].astype(jnp.bfloat16), "rows", 1).astype(
        jnp.float32
    )
    own_terms = spread[num_blocks : 2 * num_blocks] + from_above + from_below
    own_total = partner_sum(own_terms)
    feature_grad = own_total.reshape(rows_here, feat_width).astype(jnp.bfloat16)
    return (activations, feature_grad, weight_grad, bias_grad)


def solution(mesh):
    placed = (
        P("rows", None),
        P("rows", "rep", None, None),
        P("rows", "rep"),
        P("rows", "rep"),
        P(),
        P(),
        P("rows", None),
    )
    return jax.shard_map(
        local,
        mesh=mesh,
        in_specs=placed,
        out_specs=(P("rows", None), P("rows", None), P(), P()),
        check_vma=False,
    )
```

```python
import math

import jax
import jax.numpy as jnp
from jax import lax
from jax.sharding import PartitionSpec as P


def extended(block, sides, width):
    for axis, dim in sides:
        count = lax.axis_size(axis)
        forward = [(i, i + 1) for i in range(count - 1)]
        backward = [(target, source) for source, target in forward]
        low = lax.ppermute(
            lax.slice_in_dim(block, block.shape[dim] - width, None, axis=dim), axis, forward
        )
        high = lax.ppermute(lax.slice_in_dim(block, 0, width, axis=dim), axis, backward)
        block = jnp.concatenate([low, block, high], axis=dim)
    return block


def from_behind(x, axis, by):
    count = lax.axis_size(axis)
    pairs = [(i, i + by) for i in range(count) if 0 <= i + by < count]
    return lax.ppermute(x, axis, pairs)


ROW_AXES = {384: ((96, 4), (8, 12), (2, 4), (1, 2))}


def moved(x, axis, count, stride, size, target):
    pairs = []
    for index in range(count):
        coord = (index // stride) % size
        pairs.append((index, index + (target(coord) - coord) * stride))
    return lax.ppermute(x, axis, pairs)


def swapped_sum(x, axis, count, stride, size, bit):
    return x + moved(x, axis, count, stride, size, lambda c: c ^ bit)


def three_way_sum(x, axis, count, stride, size):
    third = size // 3
    ahead = moved(x, axis, count, stride, size, lambda c: (c + third) % size)
    behind = moved(x, axis, count, stride, size, lambda c: (c - third) % size)
    group = (lax.axis_index(axis) // stride) % size // third
    first = jnp.where(group == 0, x, jnp.where(group == 1, ahead, behind))
    second = jnp.where(group == 0, behind, jnp.where(group == 1, x, ahead))
    third_part = jnp.where(group == 0, ahead, jnp.where(group == 1, behind, x))
    return (first + second) + third_part


def global_sum(x, tie):
    count = lax.axis_size("rows")
    if count not in ROW_AXES or lax.axis_size("rep") != 2:
        return lax.psum(x, ("rows", "rep")), tie
    (x_stride, x_size), (z_stride, z_size), (y_stride, y_size), (c_stride, c_size) = ROW_AXES[count]
    core = (lax.axis_index("rows") // c_stride) % c_size
    width = x.shape[1] // 2
    keep = lax.dynamic_slice_in_dim(x, core * width, width, 1)
    give = lax.dynamic_slice_in_dim(x, (1 - core) * width, width, 1)
    x = keep + moved(give, "rows", count, c_stride, c_size, lambda c: c ^ 1)
    x = swapped_sum(x, "rows", count, y_stride, y_size, 1)
    x = swapped_sum(x, "rows", count, y_stride, y_size, 2)
    x = x + lax.ppermute(x, "rep", [(0, 1), (1, 0)])
    x = swapped_sum(x, "rows", count, x_stride, x_size, 1)
    x = swapped_sum(x, "rows", count, x_stride, x_size, 2)
    x, tie = lax.optimization_barrier((x, tie))
    x = swapped_sum(x, "rows", count, z_stride, z_size, 1)
    x = swapped_sum(x, "rows", count, z_stride, z_size, 2)
    x = three_way_sum(x, "rows", count, z_stride, z_size)
    other = moved(x, "rows", count, c_stride, c_size, lambda c: c ^ 1)
    joined = jnp.where(core == 0, jnp.concatenate([x, other], 1), jnp.concatenate([other, x], 1))
    return joined, tie


def partner_swap(x):
    return lax.ppermute(x, "rep", [(0, 1), (1, 0)])


def in_order(mine, theirs, partner):
    return jnp.where(
        partner == 0, jnp.concatenate([mine, theirs], 0), jnp.concatenate([theirs, mine], 0)
    )


def partner_sum(x):
    return x + lax.ppermute(x, "rep", [(0, 1), (1, 0)])


def dense_part(aggregated, grad_input, weight, bias):
    pre_act = jnp.dot(aggregated, weight, preferred_element_type=jnp.float32) + bias
    outputs = jax.nn.silu(pre_act).astype(jnp.bfloat16)
    sigmoid_pre = jax.nn.sigmoid(pre_act)
    pre_grad = (
        grad_input.astype(jnp.float32) * sigmoid_pre * (1.0 + pre_act * (1.0 - sigmoid_pre))
    ).astype(jnp.bfloat16)
    agg_grad = jnp.dot(pre_grad, weight.T, preferred_element_type=jnp.float32).astype(jnp.bfloat16)
    return (outputs, pre_grad, agg_grad)


def local(features, tiles, columns, live, weight, bias, cotangent):
    num_blocks = tiles.shape[0]
    slot_count = tiles.shape[1]
    tile_size = tiles.shape[2]
    feat_width = features.shape[1]
    rows_here = num_blocks * tile_size
    half_rows = rows_here // 2
    row_index = lax.axis_index("rows")
    partner = lax.axis_index("rep")
    node_count = rows_here * lax.axis_size("rows")
    padded = extended(features, (("rows", 0),), rows_here)
    padded_blocks = padded.reshape(3 * num_blocks, tile_size, feat_width)
    local_cols = columns - (row_index - 1) * num_blocks
    live_mask = jnp.arange(slot_count, dtype=jnp.int32)[None, :] < live
    targets = jnp.arange(3 * num_blocks, dtype=jnp.int32)
    selector = (local_cols[:, :, None] == targets[None, None, :]) & live_mask[:, :, None]
    selector = selector.astype(jnp.bfloat16)
    band_tiles = jnp.einsum(
        "bks,bkij->bsij", selector, tiles, preferred_element_type=jnp.float32
    ).astype(jnp.bfloat16)
    partial_sum = jnp.einsum(
        "bsij,sjf->bif", band_tiles, padded_blocks, preferred_element_type=jnp.float32
    )
    partial_sum = partial_sum.reshape(rows_here, feat_width)
    own_part = lax.dynamic_slice_in_dim(partial_sum, partner * half_rows, half_rows, 0)
    their_part = lax.dynamic_slice_in_dim(partial_sum, (1 - partner) * half_rows, half_rows, 0)
    agg_half = (own_part + partner_swap(their_part)).astype(jnp.bfloat16)
    grad_in = lax.dynamic_slice_in_dim(cotangent, partner * half_rows, half_rows, 0)
    act_half, grad_half, agg_grad_half = dense_part(agg_half, grad_in, weight, bias)
    sent = partner_swap(jnp.concatenate([act_half, agg_grad_half], 1))
    activations = in_order(act_half, sent[:, :feat_width], partner)
    agg_grad = in_order(agg_grad_half, sent[:, feat_width:], partner)
    weight_part = lax.dot_general(
        agg_half, grad_half, (((0,), (0,)), ((), ())), preferred_element_type=jnp.float32
    )
    bias_part = jnp.sum(grad_half.astype(jnp.float32), axis=0)
    grad_blocks = agg_grad.reshape(num_blocks, tile_size, feat_width)
    spread = jnp.einsum(
        "bsij,bif->sjf", band_tiles, grad_blocks, preferred_element_type=jnp.float32
    )
    from_above = from_behind(spread[:num_blocks], "rows", -1)
    from_below = from_behind(spread[2 * num_blocks :].astype(jnp.bfloat16), "rows", 1).astype(
        jnp.float32
    )
    own_terms = spread[num_blocks : 2 * num_blocks] + from_above + from_below
    own_total = partner_sum(own_terms)
    grad_terms, own_total = global_sum(
        jnp.concatenate([weight_part, bias_part[None, :]], axis=0), own_total
    )
    weight_total = grad_terms[:feat_width]
    bias_total = grad_terms[feat_width]
    scale = 1.0 / math.sqrt(node_count)
    weight_grad = weight_total * scale
    bias_grad = bias_total * scale
    feature_grad = own_total.reshape(rows_here, feat_width).astype(jnp.bfloat16)
    return (activations, feature_grad, weight_grad, bias_grad)


def solution(mesh):
    placed = (
        P("rows", None),
        P("rows", "rep", None, None),
        P("rows", "rep"),
        P("rows", "rep"),
        P(),
        P(),
        P("rows", None),
    )
    return jax.shard_map(
        local,
        mesh=mesh,
        in_specs=placed,
        out_specs=(P("rows", None), P("rows", None), P(), P()),
        check_vma=False,
    )
```

```python
import math

import jax
import jax.numpy as jnp
from jax import lax
from jax.sharding import PartitionSpec as P


def extended(block, sides, width):
    for axis, dim in sides:
        count = lax.axis_size(axis)
        forward = [(i, i + 1) for i in range(count - 1)]
        backward = [(target, source) for source, target in forward]
        low = lax.ppermute(
            lax.slice_in_dim(block, block.shape[dim] - width, None, axis=dim), axis, forward
        )
        high = lax.ppermute(lax.slice_in_dim(block, 0, width, axis=dim), axis, backward)
        block = jnp.concatenate([low, block, high], axis=dim)
    return block


def from_behind(x, axis, by):
    count = lax.axis_size(axis)
    pairs = [(i, i + by) for i in range(count) if 0 <= i + by < count]
    return lax.ppermute(x, axis, pairs)


ROW_AXES = {384: ((96, 4), (8, 12), (2, 4), (1, 2))}


def moved(x, axis, count, stride, size, target):
    pairs = []
    for index in range(count):
        coord = (index // stride) % size
        pairs.append((index, index + (target(coord) - coord) * stride))
    return lax.ppermute(x, axis, pairs)


def swapped_sum(x, axis, count, stride, size, bit):
    return x + moved(x, axis, count, stride, size, lambda c: c ^ bit)


def three_way_sum(x, axis, count, stride, size):
    third = size // 3
    ahead = moved(x, axis, count, stride, size, lambda c: (c + third) % size)
    behind = moved(x, axis, count, stride, size, lambda c: (c - third) % size)
    group = (lax.axis_index(axis) // stride) % size // third
    first = jnp.where(group == 0, x, jnp.where(group == 1, ahead, behind))
    second = jnp.where(group == 0, behind, jnp.where(group == 1, x, ahead))
    third_part = jnp.where(group == 0, ahead, jnp.where(group == 1, behind, x))
    return (first + second) + third_part


def global_sum(x):
    count = lax.axis_size("rows")
    if count not in ROW_AXES or lax.axis_size("rep") != 2:
        return lax.psum(x, ("rows", "rep"))
    (x_stride, x_size), (z_stride, z_size), (y_stride, y_size), (c_stride, c_size) = ROW_AXES[count]
    core = (lax.axis_index("rows") // c_stride) % c_size
    width = x.shape[1] // 2
    keep = lax.dynamic_slice_in_dim(x, core * width, width, 1)
    give = lax.dynamic_slice_in_dim(x, (1 - core) * width, width, 1)
    x = keep + moved(give, "rows", count, c_stride, c_size, lambda c: c ^ 1)
    x = swapped_sum(x, "rows", count, x_stride, x_size, 1)
    x = swapped_sum(x, "rows", count, x_stride, x_size, 2)
    x = swapped_sum(x, "rows", count, z_stride, z_size, 1)
    x = swapped_sum(x, "rows", count, z_stride, z_size, 2)
    x = three_way_sum(x, "rows", count, z_stride, z_size)
    x = swapped_sum(x, "rows", count, y_stride, y_size, 1)
    x = swapped_sum(x, "rows", count, y_stride, y_size, 2)
    x = x + lax.ppermute(x, "rep", [(0, 1), (1, 0)])
    other = moved(x, "rows", count, c_stride, c_size, lambda c: c ^ 1)
    return jnp.where(core == 0, jnp.concatenate([x, other], 1), jnp.concatenate([other, x], 1))


def partner_swap(x):
    return lax.ppermute(x, "rep", [(0, 1), (1, 0)])


def in_order(mine, theirs, partner):
    return jnp.where(
        partner == 0, jnp.concatenate([mine, theirs], 0), jnp.concatenate([theirs, mine], 0)
    )


def partner_sum(x):
    return x + lax.ppermute(x, "rep", [(0, 1), (1, 0)])


def dense_part(aggregated, grad_input, weight, bias):
    pre_act = jnp.dot(aggregated, weight, preferred_element_type=jnp.float32) + bias
    outputs = jax.nn.silu(pre_act).astype(jnp.bfloat16)
    sigmoid_pre = jax.nn.sigmoid(pre_act)
    pre_grad = (
        grad_input.astype(jnp.float32) * sigmoid_pre * (1.0 + pre_act * (1.0 - sigmoid_pre))
    ).astype(jnp.bfloat16)
    agg_grad = jnp.dot(pre_grad, weight.T, preferred_element_type=jnp.float32).astype(jnp.bfloat16)
    return (outputs, pre_grad, agg_grad)


def local(features, tiles, columns, live, weight, bias, cotangent):
    num_blocks = tiles.shape[0]
    slot_count = tiles.shape[1]
    tile_size = tiles.shape[2]
    feat_width = features.shape[1]
    rows_here = num_blocks * tile_size
    half_rows = rows_here // 2
    row_index = lax.axis_index("rows")
    partner = lax.axis_index("rep")
    node_count = rows_here * lax.axis_size("rows")
    padded = extended(features, (("rows", 0),), rows_here)
    padded_blocks = padded.reshape(3 * num_blocks, tile_size, feat_width)
    local_cols = columns - (row_index - 1) * num_blocks
    live_mask = jnp.arange(slot_count, dtype=jnp.int32)[None, :] < live
    targets = jnp.arange(3 * num_blocks, dtype=jnp.int32)
    selector = (local_cols[:, :, None] == targets[None, None, :]) & live_mask[:, :, None]
    selector = selector.astype(jnp.bfloat16)
    band_tiles = jnp.einsum(
        "bks,bkij->bsij", selector, tiles, preferred_element_type=jnp.float32
    ).astype(jnp.bfloat16)
    partial_sum = jnp.einsum(
        "bsij,sjf->bif", band_tiles, padded_blocks, preferred_element_type=jnp.float32
    )
    partial_sum = partial_sum.reshape(rows_here, feat_width)
    own_part = lax.dynamic_slice_in_dim(partial_sum, partner * half_rows, half_rows, 0)
    their_part = lax.dynamic_slice_in_dim(partial_sum, (1 - partner) * half_rows, half_rows, 0)
    agg_half = (own_part + partner_swap(their_part)).astype(jnp.bfloat16)
    grad_in = lax.dynamic_slice_in_dim(cotangent, partner * half_rows, half_rows, 0)
    act_half, grad_half, agg_grad_half = dense_part(agg_half, grad_in, weight, bias)
    sent = partner_swap(jnp.concatenate([act_half, agg_grad_half], 1))
    activations = in_order(act_half, sent[:, :feat_width], partner)
    agg_grad = in_order(agg_grad_half, sent[:, feat_width:], partner)
    weight_part = lax.dot_general(
        agg_half, grad_half, (((0,), (0,)), ((), ())), preferred_element_type=jnp.float32
    )
    bias_part = jnp.sum(grad_half.astype(jnp.float32), axis=0)
    grad_terms = global_sum(jnp.concatenate([weight_part, bias_part[None, :]], axis=0))
    weight_total = grad_terms[:feat_width]
    bias_total = grad_terms[feat_width]
    scale = 1.0 / math.sqrt(node_count)
    weight_grad = weight_total * scale
    bias_grad = bias_total * scale
    grad_blocks = agg_grad.reshape(num_blocks, tile_size, feat_width)
    spread = jnp.einsum(
        "bsij,bif->sjf", band_tiles, grad_blocks, preferred_element_type=jnp.float32
    )
    from_above = from_behind(spread[:num_blocks], "rows", -1)
    from_below = from_behind(spread[2 * num_blocks :].astype(jnp.bfloat16), "rows", 1).astype(
        jnp.float32
    )
    own_terms = spread[num_blocks : 2 * num_blocks] + from_above + from_below
    own_total = partner_sum(own_terms)
    feature_grad = own_total.reshape(rows_here, feat_width).astype(jnp.bfloat16)
    return (activations, feature_grad, weight_grad, bias_grad)


def solution(mesh):
    placed = (
        P("rows", None),
        P("rows", "rep", None, None),
        P("rows", "rep"),
        P("rows", "rep"),
        P(),
        P(),
        P("rows", None),
    )
    return jax.shard_map(
        local,
        mesh=mesh,
        in_specs=placed,
        out_specs=(P("rows", None), P("rows", None), P(), P()),
        check_vma=False,
    )
```

```python
import math

import jax
import jax.numpy as jnp
from jax import lax
from jax.sharding import PartitionSpec as P


def extended(block, sides, width):
    for axis, dim in sides:
        count = lax.axis_size(axis)
        forward = [(i, i + 1) for i in range(count - 1)]
        backward = [(target, source) for source, target in forward]
        low = lax.ppermute(
            lax.slice_in_dim(block, block.shape[dim] - width, None, axis=dim), axis, forward
        )
        high = lax.ppermute(lax.slice_in_dim(block, 0, width, axis=dim), axis, backward)
        block = jnp.concatenate([low, block, high], axis=dim)
    return block


def from_behind(x, axis, by):
    count = lax.axis_size(axis)
    pairs = [(i, i + by) for i in range(count) if 0 <= i + by < count]
    return lax.ppermute(x, axis, pairs)


ROW_AXES = {384: ((96, 4), (8, 12), (2, 4), (1, 2))}


def moved(x, axis, count, stride, size, target):
    pairs = []
    for index in range(count):
        coord = (index // stride) % size
        pairs.append((index, index + (target(coord) - coord) * stride))
    return lax.ppermute(x, axis, pairs)


def swapped_sum(x, axis, count, stride, size, bit):
    return x + moved(x, axis, count, stride, size, lambda c: c ^ bit)


def three_way_sum(x, axis, count, stride, size):
    third = size // 3
    ahead = moved(x, axis, count, stride, size, lambda c: (c + third) % size)
    behind = moved(x, axis, count, stride, size, lambda c: (c - third) % size)
    group = (lax.axis_index(axis) // stride) % size // third
    first = jnp.where(group == 0, x, jnp.where(group == 1, ahead, behind))
    second = jnp.where(group == 0, behind, jnp.where(group == 1, x, ahead))
    third_part = jnp.where(group == 0, ahead, jnp.where(group == 1, behind, x))
    return (first + second) + third_part


def chain_start(x, early):
    count = lax.axis_size("rows")
    if count not in ROW_AXES or lax.axis_size("rep") != 2:
        return x, early
    c_stride, c_size = ROW_AXES[count][3]
    core = (lax.axis_index("rows") // c_stride) % c_size
    width = x.shape[1] // 2
    keep = lax.dynamic_slice_in_dim(x, core * width, width, 1)
    give = lax.dynamic_slice_in_dim(x, (1 - core) * width, width, 1)
    x = keep + moved(give, "rows", count, c_stride, c_size, lambda c: c ^ 1)
    return lax.optimization_barrier((x, early))


def chain_next(x, mid):
    count = lax.axis_size("rows")
    if count not in ROW_AXES or lax.axis_size("rep") != 2:
        return x, mid
    x_stride, x_size = ROW_AXES[count][0]
    x = swapped_sum(x, "rows", count, x_stride, x_size, 1)
    return lax.optimization_barrier((x, mid))


def chain_rest(x, tie):
    count = lax.axis_size("rows")
    if count not in ROW_AXES or lax.axis_size("rep") != 2:
        return lax.psum(x, ("rows", "rep")), tie
    (x_stride, x_size), (z_stride, z_size), (y_stride, y_size), (c_stride, c_size) = ROW_AXES[count]
    core = (lax.axis_index("rows") // c_stride) % c_size
    x = swapped_sum(x, "rows", count, x_stride, x_size, 2)
    x = swapped_sum(x, "rows", count, z_stride, z_size, 1)
    x = swapped_sum(x, "rows", count, z_stride, z_size, 2)
    x = three_way_sum(x, "rows", count, z_stride, z_size)
    x, tie = lax.optimization_barrier((x, tie))
    x = swapped_sum(x, "rows", count, y_stride, y_size, 1)
    x = swapped_sum(x, "rows", count, y_stride, y_size, 2)
    x = x + lax.ppermute(x, "rep", [(0, 1), (1, 0)])
    other = moved(x, "rows", count, c_stride, c_size, lambda c: c ^ 1)
    joined = jnp.where(core == 0, jnp.concatenate([x, other], 1), jnp.concatenate([other, x], 1))
    return joined, tie


def partner_swap(x):
    return lax.ppermute(x, "rep", [(0, 1), (1, 0)])


def in_order(mine, theirs, partner):
    return jnp.where(
        partner == 0, jnp.concatenate([mine, theirs], 0), jnp.concatenate([theirs, mine], 0)
    )


def partner_sum(x):
    return x + lax.ppermute(x, "rep", [(0, 1), (1, 0)])


def dense_part(aggregated, grad_input, weight, bias):
    pre_act = jnp.dot(aggregated, weight, preferred_element_type=jnp.float32) + bias
    outputs = jax.nn.silu(pre_act).astype(jnp.bfloat16)
    sigmoid_pre = jax.nn.sigmoid(pre_act)
    pre_grad = (
        grad_input.astype(jnp.float32) * sigmoid_pre * (1.0 + pre_act * (1.0 - sigmoid_pre))
    ).astype(jnp.bfloat16)
    agg_grad = jnp.dot(pre_grad, weight.T, preferred_element_type=jnp.float32).astype(jnp.bfloat16)
    return (outputs, pre_grad, agg_grad)


def local(features, tiles, columns, live, weight, bias, cotangent):
    num_blocks = tiles.shape[0]
    slot_count = tiles.shape[1]
    tile_size = tiles.shape[2]
    feat_width = features.shape[1]
    rows_here = num_blocks * tile_size
    half_rows = rows_here // 2
    row_index = lax.axis_index("rows")
    partner = lax.axis_index("rep")
    node_count = rows_here * lax.axis_size("rows")
    padded = extended(features, (("rows", 0),), rows_here)
    padded_blocks = padded.reshape(3 * num_blocks, tile_size, feat_width)
    local_cols = columns - (row_index - 1) * num_blocks
    live_mask = jnp.arange(slot_count, dtype=jnp.int32)[None, :] < live
    targets = jnp.arange(3 * num_blocks, dtype=jnp.int32)
    selector = (local_cols[:, :, None] == targets[None, None, :]) & live_mask[:, :, None]
    selector = selector.astype(jnp.bfloat16)
    band_tiles = jnp.einsum(
        "bks,bkij->bsij", selector, tiles, preferred_element_type=jnp.float32
    ).astype(jnp.bfloat16)
    partial_sum = jnp.einsum(
        "bsij,sjf->bif", band_tiles, padded_blocks, preferred_element_type=jnp.float32
    )
    partial_sum = partial_sum.reshape(rows_here, feat_width)
    own_part = lax.dynamic_slice_in_dim(partial_sum, partner * half_rows, half_rows, 0)
    their_part = lax.dynamic_slice_in_dim(partial_sum, (1 - partner) * half_rows, half_rows, 0)
    agg_half = (own_part + partner_swap(their_part)).astype(jnp.bfloat16)
    grad_in = lax.dynamic_slice_in_dim(cotangent, partner * half_rows, half_rows, 0)
    act_half, grad_half, agg_grad_half = dense_part(agg_half, grad_in, weight, bias)
    weight_part = lax.dot_general(
        agg_half, grad_half, (((0,), (0,)), ((), ())), preferred_element_type=jnp.float32
    )
    bias_part = jnp.sum(grad_half.astype(jnp.float32), axis=0)
    chain, payload = chain_start(
        jnp.concatenate([weight_part, bias_part[None, :]], axis=0),
        jnp.concatenate([act_half, agg_grad_half], 1),
    )
    chain, sent = chain_next(chain, partner_swap(payload))
    activations = in_order(payload[:, :feat_width], sent[:, :feat_width], partner)
    agg_grad = in_order(payload[:, feat_width:], sent[:, feat_width:], partner)
    grad_blocks = agg_grad.reshape(num_blocks, tile_size, feat_width)
    spread = jnp.einsum(
        "bsij,bif->sjf", band_tiles, grad_blocks, preferred_element_type=jnp.float32
    )
    from_above = from_behind(spread[:num_blocks], "rows", -1)
    from_below = from_behind(spread[2 * num_blocks :].astype(jnp.bfloat16), "rows", 1).astype(
        jnp.float32
    )
    own_terms = spread[num_blocks : 2 * num_blocks] + from_above + from_below
    own_total = partner_sum(own_terms)
    grad_terms, own_total = chain_rest(chain, own_total)
    weight_total = grad_terms[:feat_width]
    bias_total = grad_terms[feat_width]
    scale = 1.0 / math.sqrt(node_count)
    weight_grad = weight_total * scale
    bias_grad = bias_total * scale
    feature_grad = own_total.reshape(rows_here, feat_width).astype(jnp.bfloat16)
    return (activations, feature_grad, weight_grad, bias_grad)


def solution(mesh):
    placed = (
        P("rows", None),
        P("rows", "rep", None, None),
        P("rows", "rep"),
        P("rows", "rep"),
        P(),
        P(),
        P("rows", None),
    )
    return jax.shard_map(
        local,
        mesh=mesh,
        in_specs=placed,
        out_specs=(P("rows", None), P("rows", None), P(), P()),
        check_vma=False,
    )
```

```python
import math

import jax
import jax.numpy as jnp
from jax import lax
from jax.sharding import PartitionSpec as P


def extended(block, sides, width):
    for axis, dim in sides:
        count = lax.axis_size(axis)
        forward = [(i, i + 1) for i in range(count - 1)]
        backward = [(target, source) for source, target in forward]
        low = lax.ppermute(
            lax.slice_in_dim(block, block.shape[dim] - width, None, axis=dim), axis, forward
        )
        high = lax.ppermute(lax.slice_in_dim(block, 0, width, axis=dim), axis, backward)
        block = jnp.concatenate([low, block, high], axis=dim)
    return block


def from_behind(x, axis, by):
    count = lax.axis_size(axis)
    pairs = [(i, i + by) for i in range(count) if 0 <= i + by < count]
    return lax.ppermute(x, axis, pairs)


ROW_AXES = {384: ((96, 4), (8, 12), (2, 4), (1, 2))}


def moved(x, axis, count, stride, size, target):
    pairs = []
    for index in range(count):
        coord = (index // stride) % size
        pairs.append((index, index + (target(coord) - coord) * stride))
    return lax.ppermute(x, axis, pairs)


def swapped_sum(x, axis, count, stride, size, bit):
    return x + moved(x, axis, count, stride, size, lambda c: c ^ bit)


def three_way_sum(x, axis, count, stride, size):
    third = size // 3
    ahead = moved(x, axis, count, stride, size, lambda c: (c + third) % size)
    behind = moved(x, axis, count, stride, size, lambda c: (c - third) % size)
    group = (lax.axis_index(axis) // stride) % size // third
    first = jnp.where(group == 0, x, jnp.where(group == 1, ahead, behind))
    second = jnp.where(group == 0, behind, jnp.where(group == 1, x, ahead))
    third_part = jnp.where(group == 0, ahead, jnp.where(group == 1, behind, x))
    return (first + second) + third_part


def global_sum(x):
    count = lax.axis_size("rows")
    if count not in ROW_AXES or lax.axis_size("rep") != 2:
        return lax.psum(x, ("rows", "rep"))
    (x_stride, x_size), (z_stride, z_size), (y_stride, y_size), (c_stride, c_size) = ROW_AXES[count]
    core = (lax.axis_index("rows") // c_stride) % c_size
    width = x.shape[1] // 2
    keep = lax.dynamic_slice_in_dim(x, core * width, width, 1)
    give = lax.dynamic_slice_in_dim(x, (1 - core) * width, width, 1)
    x = keep + moved(give, "rows", count, c_stride, c_size, lambda c: c ^ 1)
    x = swapped_sum(x, "rows", count, x_stride, x_size, 1)
    x = swapped_sum(x, "rows", count, x_stride, x_size, 2)
    x = swapped_sum(x, "rows", count, z_stride, z_size, 1)
    x = swapped_sum(x, "rows", count, z_stride, z_size, 2)
    x = three_way_sum(x, "rows", count, z_stride, z_size)
    x = swapped_sum(x, "rows", count, y_stride, y_size, 1)
    x = swapped_sum(x, "rows", count, y_stride, y_size, 2)
    x = x + lax.ppermute(x, "rep", [(0, 1), (1, 0)])
    other = moved(x, "rows", count, c_stride, c_size, lambda c: c ^ 1)
    return jnp.where(core == 0, jnp.concatenate([x, other], 1), jnp.concatenate([other, x], 1))


def partner_swap(x):
    return lax.ppermute(x, "rep", [(0, 1), (1, 0)])


def in_order(mine, theirs, partner):
    return jnp.where(
        partner == 0, jnp.concatenate([mine, theirs], 0), jnp.concatenate([theirs, mine], 0)
    )


def partner_sum(x):
    return x + lax.ppermute(x, "rep", [(0, 1), (1, 0)])


def dense_part(aggregated, grad_input, weight, bias):
    pre_act = jnp.dot(aggregated, weight, preferred_element_type=jnp.float32) + bias
    outputs = jax.nn.silu(pre_act).astype(jnp.bfloat16)
    sigmoid_pre = jax.nn.sigmoid(pre_act)
    pre_grad = (
        grad_input.astype(jnp.float32) * sigmoid_pre * (1.0 + pre_act * (1.0 - sigmoid_pre))
    ).astype(jnp.bfloat16)
    agg_grad = jnp.dot(pre_grad, weight.T, preferred_element_type=jnp.float32).astype(jnp.bfloat16)
    return (outputs, pre_grad, agg_grad)


def local(features, tiles, columns, live, weight, bias, cotangent):
    num_blocks = tiles.shape[0]
    slot_count = tiles.shape[1]
    tile_size = tiles.shape[2]
    feat_width = features.shape[1]
    rows_here = num_blocks * tile_size
    half_rows = rows_here // 2
    row_index = lax.axis_index("rows")
    partner = lax.axis_index("rep")
    node_count = rows_here * lax.axis_size("rows")
    padded = extended(features, (("rows", 0),), rows_here)
    padded_blocks = padded.reshape(3 * num_blocks, tile_size, feat_width)
    local_cols = columns - (row_index - 1) * num_blocks
    live_mask = jnp.arange(slot_count, dtype=jnp.int32)[None, :] < live
    targets = jnp.arange(3 * num_blocks, dtype=jnp.int32)
    selector = (local_cols[:, :, None] == targets[None, None, :]) & live_mask[:, :, None]
    selector = selector.astype(jnp.bfloat16)
    band_tiles = jnp.einsum(
        "bks,bkij->bsij", selector, tiles, preferred_element_type=jnp.float32
    ).astype(jnp.bfloat16)
    partial_sum = jnp.einsum(
        "bsij,sjf->bif", band_tiles, padded_blocks, preferred_element_type=jnp.float32
    )
    partial_sum = partial_sum.reshape(rows_here, feat_width)
    own_part = lax.dynamic_slice_in_dim(partial_sum, partner * half_rows, half_rows, 0)
    their_part = lax.dynamic_slice_in_dim(partial_sum, (1 - partner) * half_rows, half_rows, 0)
    agg_half = (own_part + partner_swap(their_part)).astype(jnp.bfloat16)
    grad_in = lax.dynamic_slice_in_dim(cotangent, partner * half_rows, half_rows, 0)
    act_half, grad_half, agg_grad_half = dense_part(agg_half, grad_in, weight, bias)
    sent = partner_swap(jnp.concatenate([act_half, agg_grad_half], 1))
    activations = in_order(act_half, sent[:, :feat_width], partner)
    agg_grad = in_order(agg_grad_half, sent[:, feat_width:], partner)
    weight_part = lax.dot_general(
        agg_half, grad_half, (((0,), (0,)), ((), ())), preferred_element_type=jnp.float32
    )
    bias_part = jnp.sum(grad_half.astype(jnp.float32), axis=0)
    grad_terms = global_sum(jnp.concatenate([weight_part, bias_part[None, :]], axis=0))
    weight_total = grad_terms[:feat_width]
    bias_total = grad_terms[feat_width]
    scale = 1.0 / math.sqrt(node_count)
    weight_grad = weight_total * scale
    bias_grad = bias_total * scale
    grad_blocks = agg_grad.reshape(num_blocks, tile_size, feat_width)
    spread = jnp.einsum(
        "bsij,bif->sjf", band_tiles, grad_blocks, preferred_element_type=jnp.float32
    )
    from_above = from_behind(spread[:num_blocks], "rows", -1)
    from_below = from_behind(spread[2 * num_blocks :].astype(jnp.bfloat16), "rows", 1).astype(
        jnp.float32
    )
    own_terms = spread[num_blocks : 2 * num_blocks] + from_above + from_below
    half_blocks = num_blocks // 2
    own_half = lax.dynamic_slice_in_dim(own_terms, partner * half_blocks, half_blocks, 0)
    their_half = lax.dynamic_slice_in_dim(own_terms, (1 - partner) * half_blocks, half_blocks, 0)
    total_half = (own_half + partner_swap(their_half)).astype(jnp.bfloat16)
    feature_grad = in_order(total_half, partner_swap(total_half), partner)
    feature_grad = feature_grad.reshape(rows_here, feat_width)
    return (activations, feature_grad, weight_grad, bias_grad)


def solution(mesh):
    placed = (
        P("rows", None),
        P("rows", "rep", None, None),
        P("rows", "rep"),
        P("rows", "rep"),
        P(),
        P(),
        P("rows", None),
    )
    return jax.shard_map(
        local,
        mesh=mesh,
        in_specs=placed,
        out_specs=(P("rows", None), P("rows", None), P(), P()),
        check_vma=False,
    )
```

```python
import math

import jax
import jax.numpy as jnp
from jax import lax
from jax.sharding import PartitionSpec as P


def extended(block, sides, width):
    for axis, dim in sides:
        count = lax.axis_size(axis)
        forward = [(i, i + 1) for i in range(count - 1)]
        backward = [(target, source) for source, target in forward]
        low = lax.ppermute(
            lax.slice_in_dim(block, block.shape[dim] - width, None, axis=dim), axis, forward
        )
        high = lax.ppermute(lax.slice_in_dim(block, 0, width, axis=dim), axis, backward)
        block = jnp.concatenate([low, block, high], axis=dim)
    return block


def from_behind(x, axis, by):
    count = lax.axis_size(axis)
    pairs = [(i, i + by) for i in range(count) if 0 <= i + by < count]
    return lax.ppermute(x, axis, pairs)


ROW_AXES = {384: ((96, 4), (8, 12), (2, 4), (1, 2))}


def moved(x, axis, count, stride, size, target):
    pairs = []
    for index in range(count):
        coord = (index // stride) % size
        pairs.append((index, index + (target(coord) - coord) * stride))
    return lax.ppermute(x, axis, pairs)


def swapped_sum(x, axis, count, stride, size, bit):
    return x + moved(x, axis, count, stride, size, lambda c: c ^ bit)


def three_way_sum(x, axis, count, stride, size):
    third = size // 3
    ahead = moved(x, axis, count, stride, size, lambda c: (c + third) % size)
    behind = moved(x, axis, count, stride, size, lambda c: (c - third) % size)
    group = (lax.axis_index(axis) // stride) % size // third
    first = jnp.where(group == 0, x, jnp.where(group == 1, ahead, behind))
    second = jnp.where(group == 0, behind, jnp.where(group == 1, x, ahead))
    third_part = jnp.where(group == 0, ahead, jnp.where(group == 1, behind, x))
    return (first + second) + third_part


def global_sum(x):
    count = lax.axis_size("rows")
    if count not in ROW_AXES or lax.axis_size("rep") != 2:
        return lax.psum(x, ("rows", "rep"))
    (x_stride, x_size), (z_stride, z_size), (y_stride, y_size), (c_stride, c_size) = ROW_AXES[count]
    core = (lax.axis_index("rows") // c_stride) % c_size
    width = x.shape[1] // 2
    keep = lax.dynamic_slice_in_dim(x, core * width, width, 1)
    give = lax.dynamic_slice_in_dim(x, (1 - core) * width, width, 1)
    x = keep + moved(give, "rows", count, c_stride, c_size, lambda c: c ^ 1)
    x_bit = (lax.axis_index("rows") // x_stride) % x_size % 2
    height = x.shape[0] // 2
    keep = lax.dynamic_slice_in_dim(x, x_bit * height, height, 0)
    give = lax.dynamic_slice_in_dim(x, (1 - x_bit) * height, height, 0)
    x = keep + moved(give, "rows", count, x_stride, x_size, lambda c: c ^ 1)
    x = swapped_sum(x, "rows", count, x_stride, x_size, 2)
    x = swapped_sum(x, "rows", count, z_stride, z_size, 1)
    x = swapped_sum(x, "rows", count, z_stride, z_size, 2)
    x = three_way_sum(x, "rows", count, z_stride, z_size)
    x = swapped_sum(x, "rows", count, y_stride, y_size, 1)
    x = swapped_sum(x, "rows", count, y_stride, y_size, 2)
    x = x + lax.ppermute(x, "rep", [(0, 1), (1, 0)])
    other = moved(x, "rows", count, x_stride, x_size, lambda c: c ^ 1)
    x = jnp.where(x_bit == 0, jnp.concatenate([x, other], 0), jnp.concatenate([other, x], 0))
    other = moved(x, "rows", count, c_stride, c_size, lambda c: c ^ 1)
    return jnp.where(core == 0, jnp.concatenate([x, other], 1), jnp.concatenate([other, x], 1))


def partner_swap(x):
    return lax.ppermute(x, "rep", [(0, 1), (1, 0)])


def in_order(mine, theirs, partner):
    return jnp.where(
        partner == 0, jnp.concatenate([mine, theirs], 0), jnp.concatenate([theirs, mine], 0)
    )


def partner_sum(x):
    return x + lax.ppermute(x, "rep", [(0, 1), (1, 0)])


def dense_part(aggregated, grad_input, weight, bias):
    pre_act = jnp.dot(aggregated, weight, preferred_element_type=jnp.float32) + bias
    outputs = jax.nn.silu(pre_act).astype(jnp.bfloat16)
    sigmoid_pre = jax.nn.sigmoid(pre_act)
    pre_grad = (
        grad_input.astype(jnp.float32) * sigmoid_pre * (1.0 + pre_act * (1.0 - sigmoid_pre))
    ).astype(jnp.bfloat16)
    agg_grad = jnp.dot(pre_grad, weight.T, preferred_element_type=jnp.float32).astype(jnp.bfloat16)
    return (outputs, pre_grad, agg_grad)


def local(features, tiles, columns, live, weight, bias, cotangent):
    num_blocks = tiles.shape[0]
    slot_count = tiles.shape[1]
    tile_size = tiles.shape[2]
    feat_width = features.shape[1]
    rows_here = num_blocks * tile_size
    half_rows = rows_here // 2
    row_index = lax.axis_index("rows")
    partner = lax.axis_index("rep")
    node_count = rows_here * lax.axis_size("rows")
    padded = extended(features, (("rows", 0),), rows_here)
    padded_blocks = padded.reshape(3 * num_blocks, tile_size, feat_width)
    local_cols = columns - (row_index - 1) * num_blocks
    live_mask = jnp.arange(slot_count, dtype=jnp.int32)[None, :] < live
    targets = jnp.arange(3 * num_blocks, dtype=jnp.int32)
    selector = (local_cols[:, :, None] == targets[None, None, :]) & live_mask[:, :, None]
    selector = selector.astype(jnp.bfloat16)
    band_tiles = jnp.einsum(
        "bks,bkij->bsij", selector, tiles, preferred_element_type=jnp.float32
    ).astype(jnp.bfloat16)
    partial_sum = jnp.einsum(
        "bsij,sjf->bif", band_tiles, padded_blocks, preferred_element_type=jnp.float32
    )
    partial_sum = partial_sum.reshape(rows_here, feat_width)
    own_part = lax.dynamic_slice_in_dim(partial_sum, partner * half_rows, half_rows, 0)
    their_part = lax.dynamic_slice_in_dim(partial_sum, (1 - partner) * half_rows, half_rows, 0)
    agg_half = (own_part + partner_swap(their_part)).astype(jnp.bfloat16)
    grad_in = lax.dynamic_slice_in_dim(cotangent, partner * half_rows, half_rows, 0)
    act_half, grad_half, agg_grad_half = dense_part(agg_half, grad_in, weight, bias)
    sent = partner_swap(jnp.concatenate([act_half, agg_grad_half], 1))
    activations = in_order(act_half, sent[:, :feat_width], partner)
    agg_grad = in_order(agg_grad_half, sent[:, feat_width:], partner)
    weight_part = lax.dot_general(
        agg_half, grad_half, (((0,), (0,)), ((), ())), preferred_element_type=jnp.float32
    )
    bias_part = jnp.sum(grad_half.astype(jnp.float32), axis=0)
    spare_rows = jnp.zeros((15, feat_width), jnp.float32)
    grad_terms = global_sum(jnp.concatenate([weight_part, bias_part[None, :], spare_rows], axis=0))
    weight_total = grad_terms[:feat_width]
    bias_total = grad_terms[feat_width]
    scale = 1.0 / math.sqrt(node_count)
    weight_grad = weight_total * scale
    bias_grad = bias_total * scale
    grad_blocks = agg_grad.reshape(num_blocks, tile_size, feat_width)
    spread = jnp.einsum(
        "bsij,bif->sjf", band_tiles, grad_blocks, preferred_element_type=jnp.float32
    )
    from_above = from_behind(spread[:num_blocks], "rows", -1)
    from_below = from_behind(spread[2 * num_blocks :].astype(jnp.bfloat16), "rows", 1).astype(
        jnp.float32
    )
    own_terms = spread[num_blocks : 2 * num_blocks] + from_above + from_below
    own_total = partner_sum(own_terms)
    feature_grad = own_total.reshape(rows_here, feat_width).astype(jnp.bfloat16)
    return (activations, feature_grad, weight_grad, bias_grad)


def solution(mesh):
    placed = (
        P("rows", None),
        P("rows", "rep", None, None),
        P("rows", "rep"),
        P("rows", "rep"),
        P(),
        P(),
        P("rows", None),
    )
    return jax.shard_map(
        local,
        mesh=mesh,
        in_specs=placed,
        out_specs=(P("rows", None), P("rows", None), P(), P()),
        check_vma=False,
    )
```

```python
import math

import jax
import jax.numpy as jnp
from jax import lax
from jax.sharding import PartitionSpec as P


def extended(block, sides, width):
    for axis, dim in sides:
        count = lax.axis_size(axis)
        forward = [(i, i + 1) for i in range(count - 1)]
        backward = [(target, source) for source, target in forward]
        low = lax.ppermute(
            lax.slice_in_dim(block, block.shape[dim] - width, None, axis=dim), axis, forward
        )
        high = lax.ppermute(lax.slice_in_dim(block, 0, width, axis=dim), axis, backward)
        block = jnp.concatenate([low, block, high], axis=dim)
    return block


def from_behind(x, axis, by):
    count = lax.axis_size(axis)
    pairs = [(i, i + by) for i in range(count) if 0 <= i + by < count]
    return lax.ppermute(x, axis, pairs)


ROW_AXES = {384: ((96, 4), (8, 12), (2, 4), (1, 2))}


def moved(x, axis, count, stride, size, target):
    pairs = []
    for index in range(count):
        coord = (index // stride) % size
        pairs.append((index, index + (target(coord) - coord) * stride))
    return lax.ppermute(x, axis, pairs)


def swapped_sum(x, axis, count, stride, size, bit):
    return x + moved(x, axis, count, stride, size, lambda c: c ^ bit)


def three_way_sum(x, axis, count, stride, size):
    third = size // 3
    ahead = moved(x, axis, count, stride, size, lambda c: (c + third) % size)
    behind = moved(x, axis, count, stride, size, lambda c: (c - third) % size)
    group = (lax.axis_index(axis) // stride) % size // third
    first = jnp.where(group == 0, x, jnp.where(group == 1, ahead, behind))
    second = jnp.where(group == 0, behind, jnp.where(group == 1, x, ahead))
    third_part = jnp.where(group == 0, ahead, jnp.where(group == 1, behind, x))
    return (first + second) + third_part


def global_sum(x):
    count = lax.axis_size("rows")
    if count not in ROW_AXES or lax.axis_size("rep") != 2:
        return lax.psum(x, ("rows", "rep"))
    (x_stride, x_size), (z_stride, z_size), (y_stride, y_size), (c_stride, c_size) = ROW_AXES[count]
    core = (lax.axis_index("rows") // c_stride) % c_size
    width = x.shape[1] // 2
    keep = lax.dynamic_slice_in_dim(x, core * width, width, 1)
    give = lax.dynamic_slice_in_dim(x, (1 - core) * width, width, 1)
    x = keep + moved(give, "rows", count, c_stride, c_size, lambda c: c ^ 1)
    x = swapped_sum(x, "rows", count, x_stride, x_size, 1)
    x = swapped_sum(x, "rows", count, x_stride, x_size, 2)
    x = swapped_sum(x, "rows", count, z_stride, z_size, 1)
    x = swapped_sum(x, "rows", count, z_stride, z_size, 2)
    x = three_way_sum(x, "rows", count, z_stride, z_size)
    x = swapped_sum(x, "rows", count, y_stride, y_size, 1)
    x = swapped_sum(x, "rows", count, y_stride, y_size, 2)
    x = x + lax.ppermute(x, "rep", [(0, 1), (1, 0)])
    other = moved(x, "rows", count, c_stride, c_size, lambda c: c ^ 1)
    return jnp.where(core == 0, jnp.concatenate([x, other], 1), jnp.concatenate([other, x], 1))


def partner_swap(x):
    return lax.ppermute(x, "rep", [(0, 1), (1, 0)])


def in_order(mine, theirs, partner):
    return jnp.where(
        partner == 0, jnp.concatenate([mine, theirs], 0), jnp.concatenate([theirs, mine], 0)
    )


def partner_sum(x):
    return x + lax.ppermute(x, "rep", [(0, 1), (1, 0)])


def dense_part(aggregated, grad_input, weight, bias):
    pre_act = jnp.dot(aggregated, weight, preferred_element_type=jnp.float32) + bias
    outputs = jax.nn.silu(pre_act).astype(jnp.bfloat16)
    sigmoid_pre = jax.nn.sigmoid(pre_act)
    pre_grad = (
        grad_input.astype(jnp.float32) * sigmoid_pre * (1.0 + pre_act * (1.0 - sigmoid_pre))
    ).astype(jnp.bfloat16)
    agg_grad = jnp.dot(pre_grad, weight.T, preferred_element_type=jnp.float32).astype(jnp.bfloat16)
    return (outputs, pre_grad, agg_grad)


def local(features, tiles, columns, live, weight, bias, cotangent):
    num_blocks = tiles.shape[0]
    slot_count = tiles.shape[1]
    tile_size = tiles.shape[2]
    feat_width = features.shape[1]
    rows_here = num_blocks * tile_size
    half_rows = rows_here // 2
    row_index = lax.axis_index("rows")
    partner = lax.axis_index("rep")
    node_count = rows_here * lax.axis_size("rows")
    padded = extended(features, (("rows", 0),), rows_here)
    padded_blocks = padded.reshape(3 * num_blocks, tile_size, feat_width)
    local_cols = columns - (row_index - 1) * num_blocks
    live_mask = jnp.arange(slot_count, dtype=jnp.int32)[None, :] < live
    targets = jnp.arange(3 * num_blocks, dtype=jnp.int32)
    selector = (local_cols[:, :, None] == targets[None, None, :]) & live_mask[:, :, None]
    selector = selector.astype(jnp.bfloat16)
    band_tiles = jnp.einsum(
        "bks,bkij->bsij", selector, tiles, preferred_element_type=jnp.float32
    ).astype(jnp.bfloat16)
    partial_sum = jnp.einsum(
        "bsij,sjf->bif", band_tiles, padded_blocks, preferred_element_type=jnp.float32
    )
    partial_sum = partial_sum.reshape(rows_here, feat_width)
    own_part = lax.dynamic_slice_in_dim(partial_sum, partner * half_rows, half_rows, 0)
    their_part = lax.dynamic_slice_in_dim(partial_sum, (1 - partner) * half_rows, half_rows, 0)
    their_sent = partner_swap(their_part.astype(jnp.bfloat16))
    agg_half = (own_part + their_sent.astype(jnp.float32)).astype(jnp.bfloat16)
    grad_in = lax.dynamic_slice_in_dim(cotangent, partner * half_rows, half_rows, 0)
    act_half, grad_half, agg_grad_half = dense_part(agg_half, grad_in, weight, bias)
    sent = partner_swap(jnp.concatenate([act_half, agg_grad_half], 1))
    activations = in_order(act_half, sent[:, :feat_width], partner)
    agg_grad = in_order(agg_grad_half, sent[:, feat_width:], partner)
    weight_part = lax.dot_general(
        agg_half, grad_half, (((0,), (0,)), ((), ())), preferred_element_type=jnp.float32
    )
    bias_part = jnp.sum(grad_half.astype(jnp.float32), axis=0)
    grad_terms = global_sum(jnp.concatenate([weight_part, bias_part[None, :]], axis=0))
    weight_total = grad_terms[:feat_width]
    bias_total = grad_terms[feat_width]
    scale = 1.0 / math.sqrt(node_count)
    weight_grad = weight_total * scale
    bias_grad = bias_total * scale
    grad_blocks = agg_grad.reshape(num_blocks, tile_size, feat_width)
    spread = jnp.einsum(
        "bsij,bif->sjf", band_tiles, grad_blocks, preferred_element_type=jnp.float32
    )
    from_above = from_behind(spread[:num_blocks], "rows", -1)
    from_below = from_behind(spread[2 * num_blocks :].astype(jnp.bfloat16), "rows", 1).astype(
        jnp.float32
    )
    own_terms = spread[num_blocks : 2 * num_blocks] + from_above + from_below
    own_total = partner_sum(own_terms)
    feature_grad = own_total.reshape(rows_here, feat_width).astype(jnp.bfloat16)
    return (activations, feature_grad, weight_grad, bias_grad)


def solution(mesh):
    placed = (
        P("rows", None),
        P("rows", "rep", None, None),
        P("rows", "rep"),
        P("rows", "rep"),
        P(),
        P(),
        P("rows", None),
    )
    return jax.shard_map(
        local,
        mesh=mesh,
        in_specs=placed,
        out_specs=(P("rows", None), P("rows", None), P(), P()),
        check_vma=False,
    )
```

```python
import math

import jax
import jax.numpy as jnp
from jax import lax
from jax.sharding import PartitionSpec as P


def extended(block, sides, width):
    for axis, dim in sides:
        count = lax.axis_size(axis)
        forward = [(i, i + 1) for i in range(count - 1)]
        backward = [(target, source) for source, target in forward]
        low = lax.ppermute(
            lax.slice_in_dim(block, block.shape[dim] - width, None, axis=dim), axis, forward
        )
        high = lax.ppermute(lax.slice_in_dim(block, 0, width, axis=dim), axis, backward)
        block = jnp.concatenate([low, block, high], axis=dim)
    return block


def from_behind(x, axis, by):
    count = lax.axis_size(axis)
    pairs = [(i, i + by) for i in range(count) if 0 <= i + by < count]
    return lax.ppermute(x, axis, pairs)


ROW_AXES = {384: ((96, 4), (8, 12), (2, 4), (1, 2))}


def moved(x, axis, count, stride, size, target):
    pairs = []
    for index in range(count):
        coord = (index // stride) % size
        pairs.append((index, index + (target(coord) - coord) * stride))
    return lax.ppermute(x, axis, pairs)


def swapped_sum(x, axis, count, stride, size, bit):
    return x + moved(x, axis, count, stride, size, lambda c: c ^ bit)


def ring_sum(x, axis, count, stride, size):
    coord = (lax.axis_index(axis) // stride) % size
    parts = [x] + [
        moved(x, axis, count, stride, size, lambda c, k=k: (c - k) % size) for k in range(1, size)
    ]
    stacked = jnp.stack(parts)
    total = lax.dynamic_index_in_dim(stacked, (0 - coord) % size, 0, keepdims=False)
    for position in range(1, size):
        total = total + lax.dynamic_index_in_dim(stacked, (position - coord) % size, 0, keepdims=False)
    return total


def three_way_sum(x, axis, count, stride, size):
    third = size // 3
    ahead = moved(x, axis, count, stride, size, lambda c: (c + third) % size)
    behind = moved(x, axis, count, stride, size, lambda c: (c - third) % size)
    group = (lax.axis_index(axis) // stride) % size // third
    first = jnp.where(group == 0, x, jnp.where(group == 1, ahead, behind))
    second = jnp.where(group == 0, behind, jnp.where(group == 1, x, ahead))
    third_part = jnp.where(group == 0, ahead, jnp.where(group == 1, behind, x))
    return (first + second) + third_part


def global_sum(x):
    count = lax.axis_size("rows")
    if count not in ROW_AXES or lax.axis_size("rep") != 2:
        return lax.psum(x, ("rows", "rep"))
    (x_stride, x_size), (z_stride, z_size), (y_stride, y_size), (c_stride, c_size) = ROW_AXES[count]
    core = (lax.axis_index("rows") // c_stride) % c_size
    width = x.shape[1] // 2
    keep = lax.dynamic_slice_in_dim(x, core * width, width, 1)
    give = lax.dynamic_slice_in_dim(x, (1 - core) * width, width, 1)
    x = keep + moved(give, "rows", count, c_stride, c_size, lambda c: c ^ 1)
    x = ring_sum(x, "rows", count, x_stride, x_size)
    x = swapped_sum(x, "rows", count, z_stride, z_size, 1)
    x = swapped_sum(x, "rows", count, z_stride, z_size, 2)
    x = three_way_sum(x, "rows", count, z_stride, z_size)
    x = swapped_sum(x, "rows", count, y_stride, y_size, 1)
    x = swapped_sum(x, "rows", count, y_stride, y_size, 2)
    x = x + lax.ppermute(x, "rep", [(0, 1), (1, 0)])
    other = moved(x, "rows", count, c_stride, c_size, lambda c: c ^ 1)
    return jnp.where(core == 0, jnp.concatenate([x, other], 1), jnp.concatenate([other, x], 1))


def partner_swap(x):
    return lax.ppermute(x, "rep", [(0, 1), (1, 0)])


def in_order(mine, theirs, partner):
    return jnp.where(
        partner == 0, jnp.concatenate([mine, theirs], 0), jnp.concatenate([theirs, mine], 0)
    )


def partner_sum(x):
    return x + lax.ppermute(x, "rep", [(0, 1), (1, 0)])


def dense_part(aggregated, grad_input, weight, bias):
    pre_act = jnp.dot(aggregated, weight, preferred_element_type=jnp.float32) + bias
    outputs = jax.nn.silu(pre_act).astype(jnp.bfloat16)
    sigmoid_pre = jax.nn.sigmoid(pre_act)
    pre_grad = (
        grad_input.astype(jnp.float32) * sigmoid_pre * (1.0 + pre_act * (1.0 - sigmoid_pre))
    ).astype(jnp.bfloat16)
    agg_grad = jnp.dot(pre_grad, weight.T, preferred_element_type=jnp.float32).astype(jnp.bfloat16)
    return (outputs, pre_grad, agg_grad)


def local(features, tiles, columns, live, weight, bias, cotangent):
    num_blocks = tiles.shape[0]
    slot_count = tiles.shape[1]
    tile_size = tiles.shape[2]
    feat_width = features.shape[1]
    rows_here = num_blocks * tile_size
    half_rows = rows_here // 2
    row_index = lax.axis_index("rows")
    partner = lax.axis_index("rep")
    node_count = rows_here * lax.axis_size("rows")
    padded = extended(features, (("rows", 0),), rows_here)
    padded_blocks = padded.reshape(3 * num_blocks, tile_size, feat_width)
    local_cols = columns - (row_index - 1) * num_blocks
    live_mask = jnp.arange(slot_count, dtype=jnp.int32)[None, :] < live
    targets = jnp.arange(3 * num_blocks, dtype=jnp.int32)
    selector = (local_cols[:, :, None] == targets[None, None, :]) & live_mask[:, :, None]
    selector = selector.astype(jnp.bfloat16)
    band_tiles = jnp.einsum(
        "bks,bkij->bsij", selector, tiles, preferred_element_type=jnp.float32
    ).astype(jnp.bfloat16)
    partial_sum = jnp.einsum(
        "bsij,sjf->bif", band_tiles, padded_blocks, preferred_element_type=jnp.float32
    )
    partial_sum = partial_sum.reshape(rows_here, feat_width)
    own_part = lax.dynamic_slice_in_dim(partial_sum, partner * half_rows, half_rows, 0)
    their_part = lax.dynamic_slice_in_dim(partial_sum, (1 - partner) * half_rows, half_rows, 0)
    their_sent = partner_swap(their_part.astype(jnp.bfloat16))
    agg_half = (own_part + their_sent.astype(jnp.float32)).astype(jnp.bfloat16)
    grad_in = lax.dynamic_slice_in_dim(cotangent, partner * half_rows, half_rows, 0)
    act_half, grad_half, agg_grad_half = dense_part(agg_half, grad_in, weight, bias)
    sent = partner_swap(jnp.concatenate([act_half, agg_grad_half], 1))
    activations = in_order(act_half, sent[:, :feat_width], partner)
    agg_grad = in_order(agg_grad_half, sent[:, feat_width:], partner)
    weight_part = lax.dot_general(
        agg_half, grad_half, (((0,), (0,)), ((), ())), preferred_element_type=jnp.float32
    )
    bias_part = jnp.sum(grad_half.astype(jnp.float32), axis=0)
    grad_terms = global_sum(jnp.concatenate([weight_part, bias_part[None, :]], axis=0))
    weight_total = grad_terms[:feat_width]
    bias_total = grad_terms[feat_width]
    scale = 1.0 / math.sqrt(node_count)
    weight_grad = weight_total * scale
    bias_grad = bias_total * scale
    grad_blocks = agg_grad.reshape(num_blocks, tile_size, feat_width)
    spread = jnp.einsum(
        "bsij,bif->sjf", band_tiles, grad_blocks, preferred_element_type=jnp.float32
    )
    from_above = from_behind(spread[:num_blocks], "rows", -1)
    from_below = from_behind(spread[2 * num_blocks :].astype(jnp.bfloat16), "rows", 1).astype(
        jnp.float32
    )
    own_terms = spread[num_blocks : 2 * num_blocks] + from_above + from_below
    own_total = partner_sum(own_terms)
    feature_grad = own_total.reshape(rows_here, feat_width).astype(jnp.bfloat16)
    return (activations, feature_grad, weight_grad, bias_grad)


def solution(mesh):
    placed = (
        P("rows", None),
        P("rows", "rep", None, None),
        P("rows", "rep"),
        P("rows", "rep"),
        P(),
        P(),
        P("rows", None),
    )
    return jax.shard_map(
        local,
        mesh=mesh,
        in_specs=placed,
        out_specs=(P("rows", None), P("rows", None), P(), P()),
        check_vma=False,
    )
```

```python
import math

import jax
import jax.numpy as jnp
from jax import lax
from jax.sharding import PartitionSpec as P


def extended(block, sides, width):
    for axis, dim in sides:
        count = lax.axis_size(axis)
        forward = [(i, i + 1) for i in range(count - 1)]
        backward = [(target, source) for source, target in forward]
        low = lax.ppermute(
            lax.slice_in_dim(block, block.shape[dim] - width, None, axis=dim), axis, forward
        )
        high = lax.ppermute(lax.slice_in_dim(block, 0, width, axis=dim), axis, backward)
        block = jnp.concatenate([low, block, high], axis=dim)
    return block


def from_behind(x, axis, by):
    count = lax.axis_size(axis)
    pairs = [(i, i + by) for i in range(count) if 0 <= i + by < count]
    return lax.ppermute(x, axis, pairs)


ROW_AXES = {384: ((96, 4), (8, 12), (2, 4), (1, 2))}


def moved(x, axis, count, stride, size, target):
    pairs = []
    for index in range(count):
        coord = (index // stride) % size
        pairs.append((index, index + (target(coord) - coord) * stride))
    return lax.ppermute(x, axis, pairs)


def swapped_sum(x, axis, count, stride, size, bit):
    return x + moved(x, axis, count, stride, size, lambda c: c ^ bit)


def ring_sum(x, axis, count, stride, size):
    coord = (lax.axis_index(axis) // stride) % size
    parts = [x] + [
        moved(x, axis, count, stride, size, lambda c, k=k: (c - k) % size) for k in range(1, size)
    ]
    stacked = jnp.stack(parts)
    total = lax.dynamic_index_in_dim(stacked, (0 - coord) % size, 0, keepdims=False)
    for position in range(1, size):
        total = total + lax.dynamic_index_in_dim(stacked, (position - coord) % size, 0, keepdims=False)
    return total


def three_way_sum(x, axis, count, stride, size):
    third = size // 3
    ahead = moved(x, axis, count, stride, size, lambda c: (c + third) % size)
    behind = moved(x, axis, count, stride, size, lambda c: (c - third) % size)
    group = (lax.axis_index(axis) // stride) % size // third
    first = jnp.where(group == 0, x, jnp.where(group == 1, ahead, behind))
    second = jnp.where(group == 0, behind, jnp.where(group == 1, x, ahead))
    third_part = jnp.where(group == 0, ahead, jnp.where(group == 1, behind, x))
    return (first + second) + third_part


def global_sum(x):
    count = lax.axis_size("rows")
    if count not in ROW_AXES or lax.axis_size("rep") != 2:
        return lax.psum(x, ("rows", "rep"))
    (x_stride, x_size), (z_stride, z_size), (y_stride, y_size), (c_stride, c_size) = ROW_AXES[count]
    core = (lax.axis_index("rows") // c_stride) % c_size
    width = x.shape[1] // 2
    keep = lax.dynamic_slice_in_dim(x, core * width, width, 1)
    give = lax.dynamic_slice_in_dim(x, (1 - core) * width, width, 1)
    x = keep + moved(give, "rows", count, c_stride, c_size, lambda c: c ^ 1)
    x = ring_sum(x, "rows", count, x_stride, x_size)
    x = ring_sum(x, "rows", count, z_stride, z_size // 3)
    x = three_way_sum(x, "rows", count, z_stride, z_size)
    x = ring_sum(x, "rows", count, y_stride, y_size)
    x = x + lax.ppermute(x, "rep", [(0, 1), (1, 0)])
    other = moved(x, "rows", count, c_stride, c_size, lambda c: c ^ 1)
    return jnp.where(core == 0, jnp.concatenate([x, other], 1), jnp.concatenate([other, x], 1))


def partner_swap(x):
    return lax.ppermute(x, "rep", [(0, 1), (1, 0)])


def in_order(mine, theirs, partner):
    return jnp.where(
        partner == 0, jnp.concatenate([mine, theirs], 0), jnp.concatenate([theirs, mine], 0)
    )


def partner_sum(x):
    return x + lax.ppermute(x, "rep", [(0, 1), (1, 0)])


def dense_part(aggregated, grad_input, weight, bias):
    pre_act = jnp.dot(aggregated, weight, preferred_element_type=jnp.float32) + bias
    outputs = jax.nn.silu(pre_act).astype(jnp.bfloat16)
    sigmoid_pre = jax.nn.sigmoid(pre_act)
    pre_grad = (
        grad_input.astype(jnp.float32) * sigmoid_pre * (1.0 + pre_act * (1.0 - sigmoid_pre))
    ).astype(jnp.bfloat16)
    agg_grad = jnp.dot(pre_grad, weight.T, preferred_element_type=jnp.float32).astype(jnp.bfloat16)
    return (outputs, pre_grad, agg_grad)


def local(features, tiles, columns, live, weight, bias, cotangent):
    num_blocks = tiles.shape[0]
    slot_count = tiles.shape[1]
    tile_size = tiles.shape[2]
    feat_width = features.shape[1]
    rows_here = num_blocks * tile_size
    half_rows = rows_here // 2
    row_index = lax.axis_index("rows")
    partner = lax.axis_index("rep")
    node_count = rows_here * lax.axis_size("rows")
    padded = extended(features, (("rows", 0),), rows_here)
    padded_blocks = padded.reshape(3 * num_blocks, tile_size, feat_width)
    local_cols = columns - (row_index - 1) * num_blocks
    live_mask = jnp.arange(slot_count, dtype=jnp.int32)[None, :] < live
    targets = jnp.arange(3 * num_blocks, dtype=jnp.int32)
    selector = (local_cols[:, :, None] == targets[None, None, :]) & live_mask[:, :, None]
    selector = selector.astype(jnp.bfloat16)
    band_tiles = jnp.einsum(
        "bks,bkij->bsij", selector, tiles, preferred_element_type=jnp.float32
    ).astype(jnp.bfloat16)
    partial_sum = jnp.einsum(
        "bsij,sjf->bif", band_tiles, padded_blocks, preferred_element_type=jnp.float32
    )
    partial_sum = partial_sum.reshape(rows_here, feat_width)
    own_part = lax.dynamic_slice_in_dim(partial_sum, partner * half_rows, half_rows, 0)
    their_part = lax.dynamic_slice_in_dim(partial_sum, (1 - partner) * half_rows, half_rows, 0)
    their_sent = partner_swap(their_part.astype(jnp.bfloat16))
    agg_half = (own_part + their_sent.astype(jnp.float32)).astype(jnp.bfloat16)
    grad_in = lax.dynamic_slice_in_dim(cotangent, partner * half_rows, half_rows, 0)
    act_half, grad_half, agg_grad_half = dense_part(agg_half, grad_in, weight, bias)
    sent = partner_swap(jnp.concatenate([act_half, agg_grad_half], 1))
    activations = in_order(act_half, sent[:, :feat_width], partner)
    agg_grad = in_order(agg_grad_half, sent[:, feat_width:], partner)
    weight_part = lax.dot_general(
        agg_half, grad_half, (((0,), (0,)), ((), ())), preferred_element_type=jnp.float32
    )
    bias_part = jnp.sum(grad_half.astype(jnp.float32), axis=0)
    grad_terms = global_sum(jnp.concatenate([weight_part, bias_part[None, :]], axis=0))
    weight_total = grad_terms[:feat_width]
    bias_total = grad_terms[feat_width]
    scale = 1.0 / math.sqrt(node_count)
    weight_grad = weight_total * scale
    bias_grad = bias_total * scale
    grad_blocks = agg_grad.reshape(num_blocks, tile_size, feat_width)
    spread = jnp.einsum(
        "bsij,bif->sjf", band_tiles, grad_blocks, preferred_element_type=jnp.float32
    )
    from_above = from_behind(spread[:num_blocks], "rows", -1)
    from_below = from_behind(spread[2 * num_blocks :].astype(jnp.bfloat16), "rows", 1).astype(
        jnp.float32
    )
    own_terms = spread[num_blocks : 2 * num_blocks] + from_above + from_below
    own_total = partner_sum(own_terms)
    feature_grad = own_total.reshape(rows_here, feat_width).astype(jnp.bfloat16)
    return (activations, feature_grad, weight_grad, bias_grad)


def solution(mesh):
    placed = (
        P("rows", None),
        P("rows", "rep", None, None),
        P("rows", "rep"),
        P("rows", "rep"),
        P(),
        P(),
        P("rows", None),
    )
    return jax.shard_map(
        local,
        mesh=mesh,
        in_specs=placed,
        out_specs=(P("rows", None), P("rows", None), P(), P()),
        check_vma=False,
    )
```

```python
import math

import jax
import jax.numpy as jnp
from jax import lax
from jax.sharding import PartitionSpec as P


def extended(block, sides, width):
    for axis, dim in sides:
        count = lax.axis_size(axis)
        forward = [(i, i + 1) for i in range(count - 1)]
        backward = [(target, source) for source, target in forward]
        low = lax.ppermute(
            lax.slice_in_dim(block, block.shape[dim] - width, None, axis=dim), axis, forward
        )
        high = lax.ppermute(lax.slice_in_dim(block, 0, width, axis=dim), axis, backward)
        block = jnp.concatenate([low, block, high], axis=dim)
    return block


def from_behind(x, axis, by):
    count = lax.axis_size(axis)
    pairs = [(i, i + by) for i in range(count) if 0 <= i + by < count]
    return lax.ppermute(x, axis, pairs)


ROW_AXES = {384: ((96, 4), (8, 12), (2, 4), (1, 2))}


def moved(x, axis, count, stride, size, target):
    pairs = []
    for index in range(count):
        coord = (index // stride) % size
        pairs.append((index, index + (target(coord) - coord) * stride))
    return lax.ppermute(x, axis, pairs)


def swapped_sum(x, axis, count, stride, size, bit):
    return x + moved(x, axis, count, stride, size, lambda c: c ^ bit)


def ring_sum(x, axis, count, stride, size):
    coord = (lax.axis_index(axis) // stride) % size
    parts = [x] + [
        moved(x, axis, count, stride, size, lambda c, k=k: (c - k) % size) for k in range(1, size)
    ]
    stacked = jnp.stack(parts)
    total = lax.dynamic_index_in_dim(stacked, (0 - coord) % size, 0, keepdims=False)
    for position in range(1, size):
        total = total + lax.dynamic_index_in_dim(stacked, (position - coord) % size, 0, keepdims=False)
    return total


def three_way_sum(x, axis, count, stride, size):
    third = size // 3
    ahead = moved(x, axis, count, stride, size, lambda c: (c + third) % size)
    behind = moved(x, axis, count, stride, size, lambda c: (c - third) % size)
    group = (lax.axis_index(axis) // stride) % size // third
    first = jnp.where(group == 0, x, jnp.where(group == 1, ahead, behind))
    second = jnp.where(group == 0, behind, jnp.where(group == 1, x, ahead))
    third_part = jnp.where(group == 0, ahead, jnp.where(group == 1, behind, x))
    return (first + second) + third_part


def global_sum(x):
    count = lax.axis_size("rows")
    if count not in ROW_AXES or lax.axis_size("rep") != 2:
        return lax.psum(x, ("rows", "rep"))
    (x_stride, x_size), (z_stride, z_size), (y_stride, y_size), (c_stride, c_size) = ROW_AXES[count]
    core = (lax.axis_index("rows") // c_stride) % c_size
    width = x.shape[1] // 2
    keep = lax.dynamic_slice_in_dim(x, core * width, width, 1)
    give = lax.dynamic_slice_in_dim(x, (1 - core) * width, width, 1)
    x = keep + moved(give, "rows", count, c_stride, c_size, lambda c: c ^ 1)
    x = ring_sum(x, "rows", count, x_stride, x_size)
    x = ring_sum(x, "rows", count, z_stride, z_size // 3)
    x = three_way_sum(x, "rows", count, z_stride, z_size)
    x = swapped_sum(x, "rows", count, y_stride, y_size, 1)
    x = swapped_sum(x, "rows", count, y_stride, y_size, 2)
    x = x + lax.ppermute(x, "rep", [(0, 1), (1, 0)])
    other = moved(x, "rows", count, c_stride, c_size, lambda c: c ^ 1)
    return jnp.where(core == 0, jnp.concatenate([x, other], 1), jnp.concatenate([other, x], 1))


def partner_swap(x):
    return lax.ppermute(x, "rep", [(0, 1), (1, 0)])


def in_order(mine, theirs, partner):
    return jnp.where(
        partner == 0, jnp.concatenate([mine, theirs], 0), jnp.concatenate([theirs, mine], 0)
    )


def partner_sum(x):
    return x + lax.ppermute(x, "rep", [(0, 1), (1, 0)])


def dense_part(aggregated, grad_input, weight, bias):
    pre_act = jnp.dot(aggregated, weight, preferred_element_type=jnp.float32) + bias
    outputs = jax.nn.silu(pre_act).astype(jnp.bfloat16)
    sigmoid_pre = jax.nn.sigmoid(pre_act)
    pre_grad = (
        grad_input.astype(jnp.float32) * sigmoid_pre * (1.0 + pre_act * (1.0 - sigmoid_pre))
    ).astype(jnp.bfloat16)
    agg_grad = jnp.dot(pre_grad, weight.T, preferred_element_type=jnp.float32).astype(jnp.bfloat16)
    return (outputs, pre_grad, agg_grad)


def local(features, tiles, columns, live, weight, bias, cotangent):
    num_blocks = tiles.shape[0]
    slot_count = tiles.shape[1]
    tile_size = tiles.shape[2]
    feat_width = features.shape[1]
    rows_here = num_blocks * tile_size
    half_rows = rows_here // 2
    row_index = lax.axis_index("rows")
    partner = lax.axis_index("rep")
    node_count = rows_here * lax.axis_size("rows")
    padded = extended(features, (("rows", 0),), rows_here)
    padded_blocks = padded.reshape(3 * num_blocks, tile_size, feat_width)
    local_cols = columns - (row_index - 1) * num_blocks
    live_mask = jnp.arange(slot_count, dtype=jnp.int32)[None, :] < live
    targets = jnp.arange(3 * num_blocks, dtype=jnp.int32)
    selector = (local_cols[:, :, None] == targets[None, None, :]) & live_mask[:, :, None]
    selector = selector.astype(jnp.bfloat16)
    band_tiles = jnp.einsum(
        "bks,bkij->bsij", selector, tiles, preferred_element_type=jnp.float32
    ).astype(jnp.bfloat16)
    partial_sum = jnp.einsum(
        "bsij,sjf->bif", band_tiles, padded_blocks, preferred_element_type=jnp.float32
    )
    partial_sum = partial_sum.reshape(rows_here, feat_width)
    own_part = lax.dynamic_slice_in_dim(partial_sum, partner * half_rows, half_rows, 0)
    their_part = lax.dynamic_slice_in_dim(partial_sum, (1 - partner) * half_rows, half_rows, 0)
    their_sent = partner_swap(their_part.astype(jnp.bfloat16))
    agg_half = (own_part + their_sent.astype(jnp.float32)).astype(jnp.bfloat16)
    grad_in = lax.dynamic_slice_in_dim(cotangent, partner * half_rows, half_rows, 0)
    act_half, grad_half, agg_grad_half = dense_part(agg_half, grad_in, weight, bias)
    sent = partner_swap(jnp.concatenate([act_half, agg_grad_half], 1))
    activations = in_order(act_half, sent[:, :feat_width], partner)
    agg_grad = in_order(agg_grad_half, sent[:, feat_width:], partner)
    weight_part = lax.dot_general(
        agg_half, grad_half, (((0,), (0,)), ((), ())), preferred_element_type=jnp.float32
    )
    bias_part = jnp.sum(grad_half.astype(jnp.float32), axis=0)
    grad_terms = global_sum(jnp.concatenate([weight_part, bias_part[None, :]], axis=0))
    weight_total = grad_terms[:feat_width]
    bias_total = grad_terms[feat_width]
    scale = 1.0 / math.sqrt(node_count)
    weight_grad = weight_total * scale
    bias_grad = bias_total * scale
    grad_blocks = agg_grad.reshape(num_blocks, tile_size, feat_width)
    spread = jnp.einsum(
        "bsij,bif->sjf", band_tiles, grad_blocks, preferred_element_type=jnp.float32
    )
    from_above = from_behind(spread[:num_blocks], "rows", -1)
    from_below = from_behind(spread[2 * num_blocks :].astype(jnp.bfloat16), "rows", 1).astype(
        jnp.float32
    )
    own_terms = spread[num_blocks : 2 * num_blocks] + from_above + from_below
    own_total = partner_sum(own_terms)
    feature_grad = own_total.reshape(rows_here, feat_width).astype(jnp.bfloat16)
    return (activations, feature_grad, weight_grad, bias_grad)


def solution(mesh):
    placed = (
        P("rows", None),
        P("rows", "rep", None, None),
        P("rows", "rep"),
        P("rows", "rep"),
        P(),
        P(),
        P("rows", None),
    )
    return jax.shard_map(
        local,
        mesh=mesh,
        in_specs=placed,
        out_specs=(P("rows", None), P("rows", None), P(), P()),
        check_vma=False,
    )
```

```python
import math

import jax
import jax.numpy as jnp
from jax import lax
from jax.sharding import PartitionSpec as P


def extended(block, sides, width):
    for axis, dim in sides:
        count = lax.axis_size(axis)
        forward = [(i, i + 1) for i in range(count - 1)]
        backward = [(target, source) for source, target in forward]
        low = lax.ppermute(
            lax.slice_in_dim(block, block.shape[dim] - width, None, axis=dim), axis, forward
        )
        high = lax.ppermute(lax.slice_in_dim(block, 0, width, axis=dim), axis, backward)
        block = jnp.concatenate([low, block, high], axis=dim)
    return block


def from_behind(x, axis, by):
    count = lax.axis_size(axis)
    pairs = [(i, i + by) for i in range(count) if 0 <= i + by < count]
    return lax.ppermute(x, axis, pairs)


ROW_AXES = {384: ((96, 4), (8, 12), (2, 4), (1, 2))}


def moved(x, axis, count, stride, size, target):
    pairs = []
    for index in range(count):
        coord = (index // stride) % size
        pairs.append((index, index + (target(coord) - coord) * stride))
    return lax.ppermute(x, axis, pairs)


def swapped_sum(x, axis, count, stride, size, bit):
    return x + moved(x, axis, count, stride, size, lambda c: c ^ bit)


def ring_sum(x, axis, count, stride, size):
    coord = (lax.axis_index(axis) // stride) % size
    parts = [x] + [
        moved(x, axis, count, stride, size, lambda c, k=k: (c - k) % size) for k in range(1, size)
    ]
    stacked = jnp.stack(parts)
    total = lax.dynamic_index_in_dim(stacked, (0 - coord) % size, 0, keepdims=False)
    for position in range(1, size):
        total = total + lax.dynamic_index_in_dim(stacked, (position - coord) % size, 0, keepdims=False)
    return total


def three_way_sum(x, axis, count, stride, size):
    third = size // 3
    ahead = moved(x, axis, count, stride, size, lambda c: (c + third) % size)
    behind = moved(x, axis, count, stride, size, lambda c: (c - third) % size)
    group = (lax.axis_index(axis) // stride) % size // third
    first = jnp.where(group == 0, x, jnp.where(group == 1, ahead, behind))
    second = jnp.where(group == 0, behind, jnp.where(group == 1, x, ahead))
    third_part = jnp.where(group == 0, ahead, jnp.where(group == 1, behind, x))
    return (first + second) + third_part


def global_sum(x):
    count = lax.axis_size("rows")
    if count not in ROW_AXES or lax.axis_size("rep") != 2:
        return lax.psum(x, ("rows", "rep"))
    (x_stride, x_size), (z_stride, z_size), (y_stride, y_size), (c_stride, c_size) = ROW_AXES[count]
    core = (lax.axis_index("rows") // c_stride) % c_size
    width = x.shape[1] // 2
    keep = lax.dynamic_slice_in_dim(x, core * width, width, 1)
    give = lax.dynamic_slice_in_dim(x, (1 - core) * width, width, 1)
    x = keep + moved(give, "rows", count, c_stride, c_size, lambda c: c ^ 1)
    x = ring_sum(x, "rows", count, x_stride, x_size)
    x = swapped_sum(x, "rows", count, y_stride, y_size, 1)
    x = swapped_sum(x, "rows", count, y_stride, y_size, 2)
    x = x + lax.ppermute(x, "rep", [(0, 1), (1, 0)])
    x = swapped_sum(x, "rows", count, z_stride, z_size, 1)
    x = swapped_sum(x, "rows", count, z_stride, z_size, 2)
    x = three_way_sum(x, "rows", count, z_stride, z_size)
    other = moved(x, "rows", count, c_stride, c_size, lambda c: c ^ 1)
    return jnp.where(core == 0, jnp.concatenate([x, other], 1), jnp.concatenate([other, x], 1))


def partner_swap(x):
    return lax.ppermute(x, "rep", [(0, 1), (1, 0)])


def in_order(mine, theirs, partner):
    return jnp.where(
        partner == 0, jnp.concatenate([mine, theirs], 0), jnp.concatenate([theirs, mine], 0)
    )


def partner_sum(x):
    return x + lax.ppermute(x, "rep", [(0, 1), (1, 0)])


def dense_part(aggregated, grad_input, weight, bias):
    pre_act = jnp.dot(aggregated, weight, preferred_element_type=jnp.float32) + bias
    outputs = jax.nn.silu(pre_act).astype(jnp.bfloat16)
    sigmoid_pre = jax.nn.sigmoid(pre_act)
    pre_grad = (
        grad_input.astype(jnp.float32) * sigmoid_pre * (1.0 + pre_act * (1.0 - sigmoid_pre))
    ).astype(jnp.bfloat16)
    agg_grad = jnp.dot(pre_grad, weight.T, preferred_element_type=jnp.float32).astype(jnp.bfloat16)
    return (outputs, pre_grad, agg_grad)


def local(features, tiles, columns, live, weight, bias, cotangent):
    num_blocks = tiles.shape[0]
    slot_count = tiles.shape[1]
    tile_size = tiles.shape[2]
    feat_width = features.shape[1]
    rows_here = num_blocks * tile_size
    half_rows = rows_here // 2
    row_index = lax.axis_index("rows")
    partner = lax.axis_index("rep")
    node_count = rows_here * lax.axis_size("rows")
    padded = extended(features, (("rows", 0),), rows_here)
    padded_blocks = padded.reshape(3 * num_blocks, tile_size, feat_width)
    local_cols = columns - (row_index - 1) * num_blocks
    live_mask = jnp.arange(slot_count, dtype=jnp.int32)[None, :] < live
    targets = jnp.arange(3 * num_blocks, dtype=jnp.int32)
    selector = (local_cols[:, :, None] == targets[None, None, :]) & live_mask[:, :, None]
    selector = selector.astype(jnp.bfloat16)
    band_tiles = jnp.einsum(
        "bks,bkij->bsij", selector, tiles, preferred_element_type=jnp.float32
    ).astype(jnp.bfloat16)
    partial_sum = jnp.einsum(
        "bsij,sjf->bif", band_tiles, padded_blocks, preferred_element_type=jnp.float32
    )
    partial_sum = partial_sum.reshape(rows_here, feat_width)
    own_part = lax.dynamic_slice_in_dim(partial_sum, partner * half_rows, half_rows, 0)
    their_part = lax.dynamic_slice_in_dim(partial_sum, (1 - partner) * half_rows, half_rows, 0)
    their_sent = partner_swap(their_part.astype(jnp.bfloat16))
    agg_half = (own_part + their_sent.astype(jnp.float32)).astype(jnp.bfloat16)
    grad_in = lax.dynamic_slice_in_dim(cotangent, partner * half_rows, half_rows, 0)
    act_half, grad_half, agg_grad_half = dense_part(agg_half, grad_in, weight, bias)
    sent = partner_swap(jnp.concatenate([act_half, agg_grad_half], 1))
    activations = in_order(act_half, sent[:, :feat_width], partner)
    agg_grad = in_order(agg_grad_half, sent[:, feat_width:], partner)
    weight_part = lax.dot_general(
        agg_half, grad_half, (((0,), (0,)), ((), ())), preferred_element_type=jnp.float32
    )
    bias_part = jnp.sum(grad_half.astype(jnp.float32), axis=0)
    grad_terms = global_sum(jnp.concatenate([weight_part, bias_part[None, :]], axis=0))
    weight_total = grad_terms[:feat_width]
    bias_total = grad_terms[feat_width]
    scale = 1.0 / math.sqrt(node_count)
    weight_grad = weight_total * scale
    bias_grad = bias_total * scale
    grad_blocks = agg_grad.reshape(num_blocks, tile_size, feat_width)
    spread = jnp.einsum(
        "bsij,bif->sjf", band_tiles, grad_blocks, preferred_element_type=jnp.float32
    )
    from_above = from_behind(spread[:num_blocks], "rows", -1)
    from_below = from_behind(spread[2 * num_blocks :].astype(jnp.bfloat16), "rows", 1).astype(
        jnp.float32
    )
    own_terms = spread[num_blocks : 2 * num_blocks] + from_above + from_below
    own_total = partner_sum(own_terms)
    feature_grad = own_total.reshape(rows_here, feat_width).astype(jnp.bfloat16)
    return (activations, feature_grad, weight_grad, bias_grad)


def solution(mesh):
    placed = (
        P("rows", None),
        P("rows", "rep", None, None),
        P("rows", "rep"),
        P("rows", "rep"),
        P(),
        P(),
        P("rows", None),
    )
    return jax.shard_map(
        local,
        mesh=mesh,
        in_specs=placed,
        out_specs=(P("rows", None), P("rows", None), P(), P()),
        check_vma=False,
    )
```

```python
import math

import jax
import jax.numpy as jnp
from jax import lax
from jax.sharding import PartitionSpec as P


def extended(block, sides, width):
    for axis, dim in sides:
        count = lax.axis_size(axis)
        forward = [(i, i + 1) for i in range(count - 1)]
        backward = [(target, source) for source, target in forward]
        low = lax.ppermute(
            lax.slice_in_dim(block, block.shape[dim] - width, None, axis=dim), axis, forward
        )
        high = lax.ppermute(lax.slice_in_dim(block, 0, width, axis=dim), axis, backward)
        block = jnp.concatenate([low, block, high], axis=dim)
    return block


def from_behind(x, axis, by):
    count = lax.axis_size(axis)
    pairs = [(i, i + by) for i in range(count) if 0 <= i + by < count]
    return lax.ppermute(x, axis, pairs)


ROW_AXES = {384: ((96, 4), (8, 12), (2, 4), (1, 2))}


def moved(x, axis, count, stride, size, target):
    pairs = []
    for index in range(count):
        coord = (index // stride) % size
        pairs.append((index, index + (target(coord) - coord) * stride))
    return lax.ppermute(x, axis, pairs)


def swapped_sum(x, axis, count, stride, size, bit):
    return x + moved(x, axis, count, stride, size, lambda c: c ^ bit)


def ring_sum(x, axis, count, stride, size):
    coord = (lax.axis_index(axis) // stride) % size
    parts = [x] + [
        moved(x, axis, count, stride, size, lambda c, k=k: (c - k) % size) for k in range(1, size)
    ]
    stacked = jnp.stack(parts)
    total = lax.dynamic_index_in_dim(stacked, (0 - coord) % size, 0, keepdims=False)
    for position in range(1, size):
        total = total + lax.dynamic_index_in_dim(stacked, (position - coord) % size, 0, keepdims=False)
    return total


def three_way_sum(x, axis, count, stride, size):
    third = size // 3
    ahead = moved(x, axis, count, stride, size, lambda c: (c + third) % size)
    behind = moved(x, axis, count, stride, size, lambda c: (c - third) % size)
    group = (lax.axis_index(axis) // stride) % size // third
    first = jnp.where(group == 0, x, jnp.where(group == 1, ahead, behind))
    second = jnp.where(group == 0, behind, jnp.where(group == 1, x, ahead))
    third_part = jnp.where(group == 0, ahead, jnp.where(group == 1, behind, x))
    return (first + second) + third_part


def global_sum(x, tie):
    count = lax.axis_size("rows")
    if count not in ROW_AXES or lax.axis_size("rep") != 2:
        return lax.psum(x, ("rows", "rep")), tie
    (x_stride, x_size), (z_stride, z_size), (y_stride, y_size), (c_stride, c_size) = ROW_AXES[count]
    core = (lax.axis_index("rows") // c_stride) % c_size
    width = x.shape[1] // 2
    keep = lax.dynamic_slice_in_dim(x, core * width, width, 1)
    give = lax.dynamic_slice_in_dim(x, (1 - core) * width, width, 1)
    x = keep + moved(give, "rows", count, c_stride, c_size, lambda c: c ^ 1)
    x = ring_sum(x, "rows", count, x_stride, x_size)
    x = swapped_sum(x, "rows", count, y_stride, y_size, 1)
    x = swapped_sum(x, "rows", count, y_stride, y_size, 2)
    x = x + lax.ppermute(x, "rep", [(0, 1), (1, 0)])
    x, tie = lax.optimization_barrier((x, tie))
    x = swapped_sum(x, "rows", count, z_stride, z_size, 1)
    x = swapped_sum(x, "rows", count, z_stride, z_size, 2)
    x = three_way_sum(x, "rows", count, z_stride, z_size)
    other = moved(x, "rows", count, c_stride, c_size, lambda c: c ^ 1)
    joined = jnp.where(core == 0, jnp.concatenate([x, other], 1), jnp.concatenate([other, x], 1))
    return joined, tie


def partner_swap(x):
    return lax.ppermute(x, "rep", [(0, 1), (1, 0)])


def in_order(mine, theirs, partner):
    return jnp.where(
        partner == 0, jnp.concatenate([mine, theirs], 0), jnp.concatenate([theirs, mine], 0)
    )


def partner_sum(x):
    return x + lax.ppermute(x, "rep", [(0, 1), (1, 0)])


def dense_part(aggregated, grad_input, weight, bias):
    pre_act = jnp.dot(aggregated, weight, preferred_element_type=jnp.float32) + bias
    outputs = jax.nn.silu(pre_act).astype(jnp.bfloat16)
    sigmoid_pre = jax.nn.sigmoid(pre_act)
    pre_grad = (
        grad_input.astype(jnp.float32) * sigmoid_pre * (1.0 + pre_act * (1.0 - sigmoid_pre))
    ).astype(jnp.bfloat16)
    agg_grad = jnp.dot(pre_grad, weight.T, preferred_element_type=jnp.float32).astype(jnp.bfloat16)
    return (outputs, pre_grad, agg_grad)


def local(features, tiles, columns, live, weight, bias, cotangent):
    num_blocks = tiles.shape[0]
    slot_count = tiles.shape[1]
    tile_size = tiles.shape[2]
    feat_width = features.shape[1]
    rows_here = num_blocks * tile_size
    half_rows = rows_here // 2
    row_index = lax.axis_index("rows")
    partner = lax.axis_index("rep")
    node_count = rows_here * lax.axis_size("rows")
    padded = extended(features, (("rows", 0),), rows_here)
    padded_blocks = padded.reshape(3 * num_blocks, tile_size, feat_width)
    local_cols = columns - (row_index - 1) * num_blocks
    live_mask = jnp.arange(slot_count, dtype=jnp.int32)[None, :] < live
    targets = jnp.arange(3 * num_blocks, dtype=jnp.int32)
    selector = (local_cols[:, :, None] == targets[None, None, :]) & live_mask[:, :, None]
    selector = selector.astype(jnp.bfloat16)
    band_tiles = jnp.einsum(
        "bks,bkij->bsij", selector, tiles, preferred_element_type=jnp.float32
    ).astype(jnp.bfloat16)
    partial_sum = jnp.einsum(
        "bsij,sjf->bif", band_tiles, padded_blocks, preferred_element_type=jnp.float32
    )
    partial_sum = partial_sum.reshape(rows_here, feat_width)
    own_part = lax.dynamic_slice_in_dim(partial_sum, partner * half_rows, half_rows, 0)
    their_part = lax.dynamic_slice_in_dim(partial_sum, (1 - partner) * half_rows, half_rows, 0)
    their_sent = partner_swap(their_part.astype(jnp.bfloat16))
    agg_half = (own_part + their_sent.astype(jnp.float32)).astype(jnp.bfloat16)
    grad_in = lax.dynamic_slice_in_dim(cotangent, partner * half_rows, half_rows, 0)
    act_half, grad_half, agg_grad_half = dense_part(agg_half, grad_in, weight, bias)
    sent = partner_swap(jnp.concatenate([act_half, agg_grad_half], 1))
    activations = in_order(act_half, sent[:, :feat_width], partner)
    agg_grad = in_order(agg_grad_half, sent[:, feat_width:], partner)
    weight_part = lax.dot_general(
        agg_half, grad_half, (((0,), (0,)), ((), ())), preferred_element_type=jnp.float32
    )
    bias_part = jnp.sum(grad_half.astype(jnp.float32), axis=0)
    grad_blocks = agg_grad.reshape(num_blocks, tile_size, feat_width)
    spread = jnp.einsum(
        "bsij,bif->sjf", band_tiles, grad_blocks, preferred_element_type=jnp.float32
    )
    from_above = from_behind(spread[:num_blocks], "rows", -1)
    from_below = from_behind(spread[2 * num_blocks :].astype(jnp.bfloat16), "rows", 1).astype(
        jnp.float32
    )
    own_terms = spread[num_blocks : 2 * num_blocks] + from_above + from_below
    grad_terms, own_terms = global_sum(
        jnp.concatenate([weight_part, bias_part[None, :]], axis=0), own_terms
    )
    weight_total = grad_terms[:feat_width]
    bias_total = grad_terms[feat_width]
    scale = 1.0 / math.sqrt(node_count)
    weight_grad = weight_total * scale
    bias_grad = bias_total * scale
    own_total = partner_sum(own_terms)
    feature_grad = own_total.reshape(rows_here, feat_width).astype(jnp.bfloat16)
    return (activations, feature_grad, weight_grad, bias_grad)


def solution(mesh):
    placed = (
        P("rows", None),
        P("rows", "rep", None, None),
        P("rows", "rep"),
        P("rows", "rep"),
        P(),
        P(),
        P("rows", None),
    )
    return jax.shard_map(
        local,
        mesh=mesh,
        in_specs=placed,
        out_specs=(P("rows", None), P("rows", None), P(), P()),
        check_vma=False,
    )
```

```python
import math

import jax
import jax.numpy as jnp
from jax import lax
from jax.sharding import PartitionSpec as P


def extended(block, sides, width):
    for axis, dim in sides:
        count = lax.axis_size(axis)
        forward = [(i, i + 1) for i in range(count - 1)]
        backward = [(target, source) for source, target in forward]
        low = lax.ppermute(
            lax.slice_in_dim(block, block.shape[dim] - width, None, axis=dim), axis, forward
        )
        high = lax.ppermute(lax.slice_in_dim(block, 0, width, axis=dim), axis, backward)
        block = jnp.concatenate([low, block, high], axis=dim)
    return block


def from_behind(x, axis, by):
    count = lax.axis_size(axis)
    pairs = [(i, i + by) for i in range(count) if 0 <= i + by < count]
    return lax.ppermute(x, axis, pairs)


ROW_AXES = {384: ((96, 4), (8, 12), (2, 4), (1, 2))}


def moved(x, axis, count, stride, size, target):
    pairs = []
    for index in range(count):
        coord = (index // stride) % size
        pairs.append((index, index + (target(coord) - coord) * stride))
    return lax.ppermute(x, axis, pairs)


def swapped_sum(x, axis, count, stride, size, bit):
    return x + moved(x, axis, count, stride, size, lambda c: c ^ bit)


def ring_sum(x, axis, count, stride, size):
    coord = (lax.axis_index(axis) // stride) % size
    parts = [x] + [
        moved(x, axis, count, stride, size, lambda c, k=k: (c - k) % size) for k in range(1, size)
    ]
    stacked = jnp.stack(parts)
    total = lax.dynamic_index_in_dim(stacked, (0 - coord) % size, 0, keepdims=False)
    for position in range(1, size):
        total = total + lax.dynamic_index_in_dim(stacked, (position - coord) % size, 0, keepdims=False)
    return total


def three_way_sum(x, axis, count, stride, size):
    third = size // 3
    ahead = moved(x, axis, count, stride, size, lambda c: (c + third) % size)
    behind = moved(x, axis, count, stride, size, lambda c: (c - third) % size)
    group = (lax.axis_index(axis) // stride) % size // third
    first = jnp.where(group == 0, x, jnp.where(group == 1, ahead, behind))
    second = jnp.where(group == 0, behind, jnp.where(group == 1, x, ahead))
    third_part = jnp.where(group == 0, ahead, jnp.where(group == 1, behind, x))
    return (first + second) + third_part


def global_sum(x, tie):
    count = lax.axis_size("rows")
    if count not in ROW_AXES or lax.axis_size("rep") != 2:
        return x, tie
    (x_stride, x_size), (z_stride, z_size), (y_stride, y_size), (c_stride, c_size) = ROW_AXES[count]
    core = (lax.axis_index("rows") // c_stride) % c_size
    width = x.shape[1] // 2
    keep = lax.dynamic_slice_in_dim(x, core * width, width, 1)
    give = lax.dynamic_slice_in_dim(x, (1 - core) * width, width, 1)
    x = keep + moved(give, "rows", count, c_stride, c_size, lambda c: c ^ 1)
    x = ring_sum(x, "rows", count, x_stride, x_size)
    x = swapped_sum(x, "rows", count, y_stride, y_size, 1)
    x = swapped_sum(x, "rows", count, y_stride, y_size, 2)
    x = x + lax.ppermute(x, "rep", [(0, 1), (1, 0)])
    x, tie = lax.optimization_barrier((x, tie))
    x = swapped_sum(x, "rows", count, z_stride, z_size, 1)
    x = swapped_sum(x, "rows", count, z_stride, z_size, 2)
    return x, tie


def global_sum_end(x, tie):
    count = lax.axis_size("rows")
    if count not in ROW_AXES or lax.axis_size("rep") != 2:
        return lax.psum(x, ("rows", "rep")), tie
    (x_stride, x_size), (z_stride, z_size), (y_stride, y_size), (c_stride, c_size) = ROW_AXES[count]
    core = (lax.axis_index("rows") // c_stride) % c_size
    x, tie = lax.optimization_barrier((x, tie))
    x = three_way_sum(x, "rows", count, z_stride, z_size)
    other = moved(x, "rows", count, c_stride, c_size, lambda c: c ^ 1)
    joined = jnp.where(core == 0, jnp.concatenate([x, other], 1), jnp.concatenate([other, x], 1))
    return joined, tie


def partner_swap(x):
    return lax.ppermute(x, "rep", [(0, 1), (1, 0)])


def in_order(mine, theirs, partner):
    return jnp.where(
        partner == 0, jnp.concatenate([mine, theirs], 0), jnp.concatenate([theirs, mine], 0)
    )


def partner_sum(x):
    return x + lax.ppermute(x, "rep", [(0, 1), (1, 0)])


def dense_part(aggregated, grad_input, weight, bias):
    pre_act = jnp.dot(aggregated, weight, preferred_element_type=jnp.float32) + bias
    outputs = jax.nn.silu(pre_act).astype(jnp.bfloat16)
    sigmoid_pre = jax.nn.sigmoid(pre_act)
    pre_grad = (
        grad_input.astype(jnp.float32) * sigmoid_pre * (1.0 + pre_act * (1.0 - sigmoid_pre))
    ).astype(jnp.bfloat16)
    agg_grad = jnp.dot(pre_grad, weight.T, preferred_element_type=jnp.float32).astype(jnp.bfloat16)
    return (outputs, pre_grad, agg_grad)


def local(features, tiles, columns, live, weight, bias, cotangent):
    num_blocks = tiles.shape[0]
    slot_count = tiles.shape[1]
    tile_size = tiles.shape[2]
    feat_width = features.shape[1]
    rows_here = num_blocks * tile_size
    half_rows = rows_here // 2
    row_index = lax.axis_index("rows")
    partner = lax.axis_index("rep")
    node_count = rows_here * lax.axis_size("rows")
    padded = extended(features, (("rows", 0),), rows_here)
    padded_blocks = padded.reshape(3 * num_blocks, tile_size, feat_width)
    local_cols = columns - (row_index - 1) * num_blocks
    live_mask = jnp.arange(slot_count, dtype=jnp.int32)[None, :] < live
    targets = jnp.arange(3 * num_blocks, dtype=jnp.int32)
    selector = (local_cols[:, :, None] == targets[None, None, :]) & live_mask[:, :, None]
    selector = selector.astype(jnp.bfloat16)
    band_tiles = jnp.einsum(
        "bks,bkij->bsij", selector, tiles, preferred_element_type=jnp.float32
    ).astype(jnp.bfloat16)
    partial_sum = jnp.einsum(
        "bsij,sjf->bif", band_tiles, padded_blocks, preferred_element_type=jnp.float32
    )
    partial_sum = partial_sum.reshape(rows_here, feat_width)
    own_part = lax.dynamic_slice_in_dim(partial_sum, partner * half_rows, half_rows, 0)
    their_part = lax.dynamic_slice_in_dim(partial_sum, (1 - partner) * half_rows, half_rows, 0)
    their_sent = partner_swap(their_part.astype(jnp.bfloat16))
    agg_half = (own_part + their_sent.astype(jnp.float32)).astype(jnp.bfloat16)
    grad_in = lax.dynamic_slice_in_dim(cotangent, partner * half_rows, half_rows, 0)
    act_half, grad_half, agg_grad_half = dense_part(agg_half, grad_in, weight, bias)
    sent = partner_swap(jnp.concatenate([act_half, agg_grad_half], 1))
    activations = in_order(act_half, sent[:, :feat_width], partner)
    agg_grad = in_order(agg_grad_half, sent[:, feat_width:], partner)
    weight_part = lax.dot_general(
        agg_half, grad_half, (((0,), (0,)), ((), ())), preferred_element_type=jnp.float32
    )
    bias_part = jnp.sum(grad_half.astype(jnp.float32), axis=0)
    grad_blocks = agg_grad.reshape(num_blocks, tile_size, feat_width)
    spread = jnp.einsum(
        "bsij,bif->sjf", band_tiles, grad_blocks, preferred_element_type=jnp.float32
    )
    from_above = from_behind(spread[:num_blocks], "rows", -1)
    from_below = from_behind(spread[2 * num_blocks :].astype(jnp.bfloat16), "rows", 1).astype(
        jnp.float32
    )
    own_terms = spread[num_blocks : 2 * num_blocks] + from_above + from_below
    chain, own_terms = global_sum(
        jnp.concatenate([weight_part, bias_part[None, :]], axis=0), own_terms
    )
    grad_terms, own_total = global_sum_end(chain, partner_sum(own_terms))
    weight_total = grad_terms[:feat_width]
    bias_total = grad_terms[feat_width]
    scale = 1.0 / math.sqrt(node_count)
    weight_grad = weight_total * scale
    bias_grad = bias_total * scale
    feature_grad = own_total.reshape(rows_here, feat_width).astype(jnp.bfloat16)
    return (activations, feature_grad, weight_grad, bias_grad)


def solution(mesh):
    placed = (
        P("rows", None),
        P("rows", "rep", None, None),
        P("rows", "rep"),
        P("rows", "rep"),
        P(),
        P(),
        P("rows", None),
    )
    return jax.shard_map(
        local,
        mesh=mesh,
        in_specs=placed,
        out_specs=(P("rows", None), P("rows", None), P(), P()),
        check_vma=False,
    )
```

```python
import math

import jax
import jax.numpy as jnp
from jax import lax
from jax.sharding import PartitionSpec as P


def extended(block, sides, width):
    for axis, dim in sides:
        count = lax.axis_size(axis)
        forward = [(i, i + 1) for i in range(count - 1)]
        backward = [(target, source) for source, target in forward]
        low = lax.ppermute(
            lax.slice_in_dim(block, block.shape[dim] - width, None, axis=dim), axis, forward
        )
        high = lax.ppermute(lax.slice_in_dim(block, 0, width, axis=dim), axis, backward)
        block = jnp.concatenate([low, block, high], axis=dim)
    return block


def from_behind(x, axis, by):
    count = lax.axis_size(axis)
    pairs = [(i, i + by) for i in range(count) if 0 <= i + by < count]
    return lax.ppermute(x, axis, pairs)


ROW_AXES = {384: ((96, 4), (8, 12), (2, 4), (1, 2))}


def moved(x, axis, count, stride, size, target):
    pairs = []
    for index in range(count):
        coord = (index // stride) % size
        pairs.append((index, index + (target(coord) - coord) * stride))
    return lax.ppermute(x, axis, pairs)


def swapped_sum(x, axis, count, stride, size, bit):
    return x + moved(x, axis, count, stride, size, lambda c: c ^ bit)


def ring_sum(x, axis, count, stride, size):
    coord = (lax.axis_index(axis) // stride) % size
    parts = [x] + [
        moved(x, axis, count, stride, size, lambda c, k=k: (c - k) % size) for k in range(1, size)
    ]
    stacked = jnp.stack(parts)
    total = lax.dynamic_index_in_dim(stacked, (0 - coord) % size, 0, keepdims=False)
    for position in range(1, size):
        total = total + lax.dynamic_index_in_dim(stacked, (position - coord) % size, 0, keepdims=False)
    return total


def three_way_sum(x, axis, count, stride, size):
    third = size // 3
    ahead = moved(x, axis, count, stride, size, lambda c: (c + third) % size)
    behind = moved(x, axis, count, stride, size, lambda c: (c - third) % size)
    group = (lax.axis_index(axis) // stride) % size // third
    first = jnp.where(group == 0, x, jnp.where(group == 1, ahead, behind))
    second = jnp.where(group == 0, behind, jnp.where(group == 1, x, ahead))
    third_part = jnp.where(group == 0, ahead, jnp.where(group == 1, behind, x))
    return (first + second) + third_part


def global_sum(x, tie):
    count = lax.axis_size("rows")
    if count not in ROW_AXES or lax.axis_size("rep") != 2:
        return lax.psum(x, ("rows", "rep")), tie
    (x_stride, x_size), (z_stride, z_size), (y_stride, y_size), (c_stride, c_size) = ROW_AXES[count]
    core = (lax.axis_index("rows") // c_stride) % c_size
    width = x.shape[1] // 2
    keep = lax.dynamic_slice_in_dim(x, core * width, width, 1)
    give = lax.dynamic_slice_in_dim(x, (1 - core) * width, width, 1)
    x = keep + moved(give, "rows", count, c_stride, c_size, lambda c: c ^ 1)
    x = ring_sum(x, "rows", count, x_stride, x_size)
    x = swapped_sum(x, "rows", count, y_stride, y_size, 1)
    x = swapped_sum(x, "rows", count, y_stride, y_size, 2)
    x = x + lax.ppermute(x, "rep", [(0, 1), (1, 0)])
    x, tie = lax.optimization_barrier((x, tie))
    x = ring_sum(x, "rows", count, z_stride, z_size // 3)
    x = three_way_sum(x, "rows", count, z_stride, z_size)
    other = moved(x, "rows", count, c_stride, c_size, lambda c: c ^ 1)
    joined = jnp.where(core == 0, jnp.concatenate([x, other], 1), jnp.concatenate([other, x], 1))
    return joined, tie


def partner_swap(x):
    return lax.ppermute(x, "rep", [(0, 1), (1, 0)])


def in_order(mine, theirs, partner):
    return jnp.where(
        partner == 0, jnp.concatenate([mine, theirs], 0), jnp.concatenate([theirs, mine], 0)
    )


def partner_sum(x):
    return x + lax.ppermute(x, "rep", [(0, 1), (1, 0)])


def dense_part(aggregated, grad_input, weight, bias):
    pre_act = jnp.dot(aggregated, weight, preferred_element_type=jnp.float32) + bias
    outputs = jax.nn.silu(pre_act).astype(jnp.bfloat16)
    sigmoid_pre = jax.nn.sigmoid(pre_act)
    pre_grad = (
        grad_input.astype(jnp.float32) * sigmoid_pre * (1.0 + pre_act * (1.0 - sigmoid_pre))
    ).astype(jnp.bfloat16)
    agg_grad = jnp.dot(pre_grad, weight.T, preferred_element_type=jnp.float32).astype(jnp.bfloat16)
    return (outputs, pre_grad, agg_grad)


def local(features, tiles, columns, live, weight, bias, cotangent):
    num_blocks = tiles.shape[0]
    slot_count = tiles.shape[1]
    tile_size = tiles.shape[2]
    feat_width = features.shape[1]
    rows_here = num_blocks * tile_size
    half_rows = rows_here // 2
    row_index = lax.axis_index("rows")
    partner = lax.axis_index("rep")
    node_count = rows_here * lax.axis_size("rows")
    padded = extended(features, (("rows", 0),), rows_here)
    padded_blocks = padded.reshape(3 * num_blocks, tile_size, feat_width)
    local_cols = columns - (row_index - 1) * num_blocks
    live_mask = jnp.arange(slot_count, dtype=jnp.int32)[None, :] < live
    targets = jnp.arange(3 * num_blocks, dtype=jnp.int32)
    selector = (local_cols[:, :, None] == targets[None, None, :]) & live_mask[:, :, None]
    selector = selector.astype(jnp.bfloat16)
    band_tiles = jnp.einsum(
        "bks,bkij->bsij", selector, tiles, preferred_element_type=jnp.float32
    ).astype(jnp.bfloat16)
    partial_sum = jnp.einsum(
        "bsij,sjf->bif", band_tiles, padded_blocks, preferred_element_type=jnp.float32
    )
    partial_sum = partial_sum.reshape(rows_here, feat_width)
    own_part = lax.dynamic_slice_in_dim(partial_sum, partner * half_rows, half_rows, 0)
    their_part = lax.dynamic_slice_in_dim(partial_sum, (1 - partner) * half_rows, half_rows, 0)
    their_sent = partner_swap(their_part.astype(jnp.bfloat16))
    agg_half = (own_part + their_sent.astype(jnp.float32)).astype(jnp.bfloat16)
    grad_in = lax.dynamic_slice_in_dim(cotangent, partner * half_rows, half_rows, 0)
    act_half, grad_half, agg_grad_half = dense_part(agg_half, grad_in, weight, bias)
    sent = partner_swap(jnp.concatenate([act_half, agg_grad_half], 1))
    activations = in_order(act_half, sent[:, :feat_width], partner)
    agg_grad = in_order(agg_grad_half, sent[:, feat_width:], partner)
    weight_part = lax.dot_general(
        agg_half, grad_half, (((0,), (0,)), ((), ())), preferred_element_type=jnp.float32
    )
    bias_part = jnp.sum(grad_half.astype(jnp.float32), axis=0)
    grad_blocks = agg_grad.reshape(num_blocks, tile_size, feat_width)
    spread = jnp.einsum(
        "bsij,bif->sjf", band_tiles, grad_blocks, preferred_element_type=jnp.float32
    )
    from_above = from_behind(spread[:num_blocks], "rows", -1)
    from_below = from_behind(spread[2 * num_blocks :].astype(jnp.bfloat16), "rows", 1).astype(
        jnp.float32
    )
    own_terms = spread[num_blocks : 2 * num_blocks] + from_above + from_below
    grad_terms, own_terms = global_sum(
        jnp.concatenate([weight_part, bias_part[None, :]], axis=0), own_terms
    )
    weight_total = grad_terms[:feat_width]
    bias_total = grad_terms[feat_width]
    scale = 1.0 / math.sqrt(node_count)
    weight_grad = weight_total * scale
    bias_grad = bias_total * scale
    own_total = partner_sum(own_terms)
    feature_grad = own_total.reshape(rows_here, feat_width).astype(jnp.bfloat16)
    return (activations, feature_grad, weight_grad, bias_grad)


def solution(mesh):
    placed = (
        P("rows", None),
        P("rows", "rep", None, None),
        P("rows", "rep"),
        P("rows", "rep"),
        P(),
        P(),
        P("rows", None),
    )
    return jax.shard_map(
        local,
        mesh=mesh,
        in_specs=placed,
        out_specs=(P("rows", None), P("rows", None), P(), P()),
        check_vma=False,
    )
```

```python
import math

import jax
import jax.numpy as jnp
from jax import lax
from jax.sharding import PartitionSpec as P


def extended(block, sides, width):
    for axis, dim in sides:
        count = lax.axis_size(axis)
        forward = [(i, i + 1) for i in range(count - 1)]
        backward = [(target, source) for source, target in forward]
        low = lax.ppermute(
            lax.slice_in_dim(block, block.shape[dim] - width, None, axis=dim), axis, forward
        )
        high = lax.ppermute(lax.slice_in_dim(block, 0, width, axis=dim), axis, backward)
        block = jnp.concatenate([low, block, high], axis=dim)
    return block


def from_behind(x, axis, by):
    count = lax.axis_size(axis)
    pairs = [(i, i + by) for i in range(count) if 0 <= i + by < count]
    return lax.ppermute(x, axis, pairs)


ROW_AXES = {384: ((96, 4), (8, 12), (2, 4), (1, 2))}


def moved(x, axis, count, stride, size, target):
    pairs = []
    for index in range(count):
        coord = (index // stride) % size
        pairs.append((index, index + (target(coord) - coord) * stride))
    return lax.ppermute(x, axis, pairs)


def swapped_sum(x, axis, count, stride, size, bit):
    return x + moved(x, axis, count, stride, size, lambda c: c ^ bit)


def ring_sum(x, axis, count, stride, size):
    coord = (lax.axis_index(axis) // stride) % size
    parts = [x] + [
        moved(x, axis, count, stride, size, lambda c, k=k: (c - k) % size) for k in range(1, size)
    ]
    stacked = jnp.stack(parts)
    total = lax.dynamic_index_in_dim(stacked, (0 - coord) % size, 0, keepdims=False)
    for position in range(1, size):
        total = total + lax.dynamic_index_in_dim(stacked, (position - coord) % size, 0, keepdims=False)
    return total


def three_way_sum(x, axis, count, stride, size):
    third = size // 3
    ahead = moved(x, axis, count, stride, size, lambda c: (c + third) % size)
    behind = moved(x, axis, count, stride, size, lambda c: (c - third) % size)
    group = (lax.axis_index(axis) // stride) % size // third
    first = jnp.where(group == 0, x, jnp.where(group == 1, ahead, behind))
    second = jnp.where(group == 0, behind, jnp.where(group == 1, x, ahead))
    third_part = jnp.where(group == 0, ahead, jnp.where(group == 1, behind, x))
    return (first + second) + third_part


def global_sum(x, tie):
    count = lax.axis_size("rows")
    if count not in ROW_AXES or lax.axis_size("rep") != 2:
        return x, tie
    (x_stride, x_size), (z_stride, z_size), (y_stride, y_size), (c_stride, c_size) = ROW_AXES[count]
    core = (lax.axis_index("rows") // c_stride) % c_size
    width = x.shape[1] // 2
    keep = lax.dynamic_slice_in_dim(x, core * width, width, 1)
    give = lax.dynamic_slice_in_dim(x, (1 - core) * width, width, 1)
    x = keep + moved(give, "rows", count, c_stride, c_size, lambda c: c ^ 1)
    x = ring_sum(x, "rows", count, x_stride, x_size)
    x = swapped_sum(x, "rows", count, y_stride, y_size, 1)
    x = swapped_sum(x, "rows", count, y_stride, y_size, 2)
    x = x + lax.ppermute(x, "rep", [(0, 1), (1, 0)])
    x, tie = lax.optimization_barrier((x, tie))
    x = swapped_sum(x, "rows", count, z_stride, z_size, 1)
    x = swapped_sum(x, "rows", count, z_stride, z_size, 2)
    x = three_way_sum(x, "rows", count, z_stride, z_size)
    return x, tie


def global_sum_end(x, tie):
    count = lax.axis_size("rows")
    if count not in ROW_AXES or lax.axis_size("rep") != 2:
        return lax.psum(x, ("rows", "rep")), tie
    (x_stride, x_size), (z_stride, z_size), (y_stride, y_size), (c_stride, c_size) = ROW_AXES[count]
    core = (lax.axis_index("rows") // c_stride) % c_size
    x, tie = lax.optimization_barrier((x, tie))
    other = moved(x, "rows", count, c_stride, c_size, lambda c: c ^ 1)
    joined = jnp.where(core == 0, jnp.concatenate([x, other], 1), jnp.concatenate([other, x], 1))
    return joined, tie


def partner_swap(x):
    return lax.ppermute(x, "rep", [(0, 1), (1, 0)])


def in_order(mine, theirs, partner):
    return jnp.where(
        partner == 0, jnp.concatenate([mine, theirs], 0), jnp.concatenate([theirs, mine], 0)
    )


def partner_sum(x):
    return x + lax.ppermute(x, "rep", [(0, 1), (1, 0)])


def dense_part(aggregated, grad_input, weight, bias):
    pre_act = jnp.dot(aggregated, weight, preferred_element_type=jnp.float32) + bias
    outputs = jax.nn.silu(pre_act).astype(jnp.bfloat16)
    sigmoid_pre = jax.nn.sigmoid(pre_act)
    pre_grad = (
        grad_input.astype(jnp.float32) * sigmoid_pre * (1.0 + pre_act * (1.0 - sigmoid_pre))
    ).astype(jnp.bfloat16)
    agg_grad = jnp.dot(pre_grad, weight.T, preferred_element_type=jnp.float32).astype(jnp.bfloat16)
    return (outputs, pre_grad, agg_grad)


def local(features, tiles, columns, live, weight, bias, cotangent):
    num_blocks = tiles.shape[0]
    slot_count = tiles.shape[1]
    tile_size = tiles.shape[2]
    feat_width = features.shape[1]
    rows_here = num_blocks * tile_size
    half_rows = rows_here // 2
    row_index = lax.axis_index("rows")
    partner = lax.axis_index("rep")
    node_count = rows_here * lax.axis_size("rows")
    padded = extended(features, (("rows", 0),), rows_here)
    padded_blocks = padded.reshape(3 * num_blocks, tile_size, feat_width)
    local_cols = columns - (row_index - 1) * num_blocks
    live_mask = jnp.arange(slot_count, dtype=jnp.int32)[None, :] < live
    targets = jnp.arange(3 * num_blocks, dtype=jnp.int32)
    selector = (local_cols[:, :, None] == targets[None, None, :]) & live_mask[:, :, None]
    selector = selector.astype(jnp.bfloat16)
    band_tiles = jnp.einsum(
        "bks,bkij->bsij", selector, tiles, preferred_element_type=jnp.float32
    ).astype(jnp.bfloat16)
    partial_sum = jnp.einsum(
        "bsij,sjf->bif", band_tiles, padded_blocks, preferred_element_type=jnp.float32
    )
    partial_sum = partial_sum.reshape(rows_here, feat_width)
    own_part = lax.dynamic_slice_in_dim(partial_sum, partner * half_rows, half_rows, 0)
    their_part = lax.dynamic_slice_in_dim(partial_sum, (1 - partner) * half_rows, half_rows, 0)
    their_sent = partner_swap(their_part.astype(jnp.bfloat16))
    agg_half = (own_part + their_sent.astype(jnp.float32)).astype(jnp.bfloat16)
    grad_in = lax.dynamic_slice_in_dim(cotangent, partner * half_rows, half_rows, 0)
    act_half, grad_half, agg_grad_half = dense_part(agg_half, grad_in, weight, bias)
    sent = partner_swap(jnp.concatenate([act_half, agg_grad_half], 1))
    activations = in_order(act_half, sent[:, :feat_width], partner)
    agg_grad = in_order(agg_grad_half, sent[:, feat_width:], partner)
    weight_part = lax.dot_general(
        agg_half, grad_half, (((0,), (0,)), ((), ())), preferred_element_type=jnp.float32
    )
    bias_part = jnp.sum(grad_half.astype(jnp.float32), axis=0)
    grad_blocks = agg_grad.reshape(num_blocks, tile_size, feat_width)
    spread = jnp.einsum(
        "bsij,bif->sjf", band_tiles, grad_blocks, preferred_element_type=jnp.float32
    )
    from_above = from_behind(spread[:num_blocks], "rows", -1)
    from_below = from_behind(spread[2 * num_blocks :].astype(jnp.bfloat16), "rows", 1).astype(
        jnp.float32
    )
    own_terms = spread[num_blocks : 2 * num_blocks] + from_above + from_below
    chain, own_terms = global_sum(
        jnp.concatenate([weight_part, bias_part[None, :]], axis=0), own_terms
    )
    grad_terms, own_total = global_sum_end(chain, partner_sum(own_terms))
    weight_total = grad_terms[:feat_width]
    bias_total = grad_terms[feat_width]
    scale = 1.0 / math.sqrt(node_count)
    weight_grad = weight_total * scale
    bias_grad = bias_total * scale
    feature_grad = own_total.reshape(rows_here, feat_width).astype(jnp.bfloat16)
    return (activations, feature_grad, weight_grad, bias_grad)


def solution(mesh):
    placed = (
        P("rows", None),
        P("rows", "rep", None, None),
        P("rows", "rep"),
        P("rows", "rep"),
        P(),
        P(),
        P("rows", None),
    )
    return jax.shard_map(
        local,
        mesh=mesh,
        in_specs=placed,
        out_specs=(P("rows", None), P("rows", None), P(), P()),
        check_vma=False,
    )
```
